256 devices in a mesh: seq: 16 (over z_lo, x), tensor: 16 (over z_hi, y, core).
Axes of the slice: x: 4, y: 4, z: 8 (z_hi: 2, z_lo: 4; z = z_hi * 4 + z_lo), core: 2. Of those that a mesh axis runs over, the one named last changes fastest.
Arguments:
- query_rows: bfloat16 [4096, 4096], P('seq', 'tensor'), may hold values from -5 to 5
- key_rows: bfloat16 [4096, 4096], P('seq', 'tensor'), may hold values from -5 to 5
- value_rows: bfloat16 [4096, 4096], P('seq', 'tensor'), may hold values from -6 to 6
- query_tan: bfloat16 [4096, 4096], P('seq', 'tensor'), may hold values from -6 to 6
- key_tan: bfloat16 [4096, 4096], P('seq', 'tensor'), may hold values from -6 to 6
- value_tan: bfloat16 [4096, 4096], P('seq', 'tensor'), may hold values from -6 to 6
- routes: int32 [4096, 32], P('seq', 'tensor'), may hold values from 0 to 4095, as said below
- out_weight: bfloat16 [4096, 4096], P('tensor'), may hold values from -0.125 to 0.125
Outputs:
- output: bfloat16 [4096, 4096], P('seq', 'tensor')
- output_tan: bfloat16 [4096, 4096], P('seq', 'tensor')
The draws below stay inside these ranges and needn't reach their ends.
Inputs may be any that keep to these rules, and one draw needn't show every extreme that they name: `routes`: each head's column holds every slot of 0 to 4095 once; slot // 256 is the token's cluster. Every aligned block of 256 tokens puts exactly 16 of its tokens into each aligned block of 256 slots, for every head.
All inputs are finite; a program needn't handle non-finite values.
Results may differ from the reference program's by a relative error of at most 0.0058.
Values may be sent and summed in bfloat16 or wider, within the bound.
No kernel may reach another device: no remote copies, remote signals or barrier semaphores. Data moves between devices by JAX's collectives and lax.ppermute only.
A program may use at most 64 MiB of HBM per device.

```python
import jax
import jax.numpy as jnp
from jax import lax

D = 4096
HEADS = 32
HEAD_SIZE = 128
CLUSTER = 256
TOK_DEV = 256
TOKENS = 4096


def paired_rows(key):
    shape = (TOKENS, HEADS, HEAD_SIZE)
    query_stream = jax.random.fold_in(key, 101)
    key_stream = jax.random.fold_in(key, 102)
    queries = jnp.clip(jax.random.normal(query_stream, shape, jnp.float32), -5.0, 5.0)
    key_vals = jnp.clip(jax.random.normal(key_stream, shape, jnp.float32), -5.0, 5.0)
    return (queries.reshape(TOKENS, HEADS * HEAD_SIZE), key_vals.reshape(TOKENS, HEADS * HEAD_SIZE))


def draw_query_rows(key, part):
    return paired_rows(key)[0].astype(jnp.bfloat16)


def draw_key_rows(key, part):
    return paired_rows(key)[1].astype(jnp.bfloat16)


def shuffled(subkey):
    return jax.random.permutation(subkey, TOK_DEV)


def route_head(key):
    groups = TOKENS // TOK_DEV
    per_peer = TOK_DEV // groups
    within = jax.vmap(shuffled)(jax.random.split(jax.random.fold_in(key, 1), groups))
    assign = jax.vmap(shuffled)(jax.random.split(jax.random.fold_in(key, 2), groups))
    target = assign // per_peer
    inside = assign % per_peer
    source = jnp.arange(groups, dtype=jnp.int32)[:, None]
    local_slot = within[target, source * per_peer + inside]
    return (target * TOK_DEV + local_slot).reshape(TOKENS)


def draw_routes(key, part):
    head_keys = jax.random.split(jax.random.fold_in(key, 7), HEADS)
    return jax.vmap(route_head)(head_keys).T.astype(jnp.int32)


def spiked(array, own_key, source, target, parts, factor):
    def block_of(axis_at):
        return (jnp.arange(array.shape[axis_at]) // (array.shape[axis_at] // parts)).reshape((-1,) + (1,) * (array.ndim - 1 - axis_at))

    one_side = jax.random.permutation(own_key, parts)[block_of(target)]
    other_side = (block_of(target) + parts // 2) % parts
    return jnp.where((block_of(source) == one_side) | (block_of(source) == other_side), factor * array, array)


def shard_levels(stream_key, shape, shards, smallest, largest):
    factor_of, own = 1.0, jax.random.fold_in(stream_key, 6)
    for position, blocks in shards:
        heights = jnp.exp(jax.random.uniform(jax.random.fold_in(own, position), (blocks,), jnp.float32, smallest / len(shards), largest / len(shards)))
        factor_of = factor_of * jnp.repeat(heights, shape[position] // blocks).reshape([-1 if axis == position else 1 for axis in range(len(shape))])
    return factor_of


def noise(rng, extent, deviation, most, cuts=(), kind=jnp.bfloat16):
    values = deviation * jax.random.normal(rng, extent, jnp.float32)
    if cuts:
        values = values * shard_levels(rng, extent, cuts, -0.22, 0.18)
    return jnp.clip(values, -most, most).astype(kind)


def gaussian_with(stream_key, extent, deviation, limit, shards, heavy, held_as=jnp.bfloat16):
    drawn = deviation * jax.random.normal(stream_key, extent, jnp.float32)
    if shards:
        drawn = drawn * shard_levels(stream_key, extent, shards, -0.22, 0.18)
    return jnp.clip(spiked(drawn, jax.random.fold_in(stream_key, 3), *heavy), -limit, limit).astype(held_as)


def setup_inputs(seed: int = 0) -> dict:
    seeds = jax.random.split(jax.random.key(seed), 9)
    query_rows = draw_query_rows(jax.random.fold_in(seeds[8], 71), 0)
    key_rows = draw_key_rows(jax.random.fold_in(seeds[8], 71), 0)
    value_rows = noise(seeds[2], (TOKENS, HEADS * HEAD_SIZE), 1.0, 6.0, ((0, 16), (1, 16)))
    query_tan = noise(seeds[3], (TOKENS, HEADS * HEAD_SIZE), 1.0, 6.0, ((0, 16), (1, 16)))
    key_tan = noise(seeds[4], (TOKENS, HEADS * HEAD_SIZE), 1.0, 6.0, ((0, 16), (1, 16)))
    value_tan = noise(seeds[5], (TOKENS, HEADS * HEAD_SIZE), 1.0, 6.0, ((0, 16), (1, 16)))
    routes = draw_routes(jax.random.fold_in(seeds[8], 71), 0)
    out_weight = gaussian_with(seeds[7], (HEADS * HEAD_SIZE, D), (HEADS * HEAD_SIZE) ** -0.5, 0.125, ((0, 16),), (0, 1, 16, 2.0))
    return {"query_rows": query_rows, "key_rows": key_rows, "value_rows": value_rows, "query_tan": query_tan, "key_tan": key_tan, "value_tan": value_tan, "routes": routes, "out_weight": out_weight}


def cluster_attend(query_c, key_c, value_c, query_cluster_gradient, key_cluster_gradient, value_cluster_gradient, where_pos):
    scaling_multiplier = HEAD_SIZE ** -0.5
    query_broadcast_rows = query_c.astype(jnp.float32)
    key_broadcast_rows = key_c.astype(jnp.float32)
    logit_scores = jnp.einsum("ojc,oic->oji", query_broadcast_rows, key_broadcast_rows) * scaling_multiplier
    score_tangent_values = (jnp.einsum("ojc,oic->oji", query_cluster_gradient.astype(jnp.float32), key_broadcast_rows)
                      + jnp.einsum("ojc,oic->oji", query_broadcast_rows, key_cluster_gradient.astype(jnp.float32))) * scaling_multiplier
    visible = where_pos[:, None, :] <= where_pos[:, :, None]
    masked = jnp.where(visible, logit_scores, -jnp.inf)
    top_score = jnp.max(masked, axis=-1, keepdims=True)
    expo = jnp.where(visible, jnp.exp(masked - top_score), 0.0)
    attn_probs = expo / jnp.sum(expo, axis=-1, keepdims=True)
    probs_half = lax.optimization_barrier(attn_probs.astype(jnp.bfloat16))
    value_broadcast_rows = value_c.astype(jnp.float32)
    probability_backward = probs_half.astype(jnp.float32)
    attended_values = jnp.einsum("rtv,rvy->rty", probability_backward, value_broadcast_rows).astype(jnp.bfloat16)
    tangent_probs = attn_probs * (score_tangent_values - jnp.sum(attn_probs * score_tangent_values, axis=-1, keepdims=True))
    tangent_halfway_term = lax.optimization_barrier(tangent_probs.astype(jnp.bfloat16))
    attended_tangent_sum = (jnp.einsum("rtv,rvy->rty", tangent_halfway_term.astype(jnp.float32), value_broadcast_rows)
                    + jnp.einsum("rtv,rvy->rty", probability_backward, value_cluster_gradient.astype(jnp.float32))).astype(jnp.bfloat16)
    return attended_values, attended_tangent_sum


def by_head(matrix):
    return matrix.reshape(TOKENS, HEADS, HEAD_SIZE).transpose(1, 0, 2)


def reference(query_rows, key_rows, value_rows, query_tan, key_tan, value_tan, routes, out_weight):
    stacked = tuple(by_head(matrix) for matrix in (query_rows, key_rows, value_rows, query_tan, key_tan, value_tan))
    clusters = TOKENS // CLUSTER

    def one_head(items):
        head_slots = items[0]
        token_order = jnp.argsort(head_slots).astype(jnp.int32)
        grouped = [matrix[token_order].reshape(clusters, CLUSTER, HEAD_SIZE) for matrix in items[1:]]
        attended_values, attended_tangent_sum = cluster_attend(*grouped, token_order.reshape(clusters, CLUSTER))
        inverse = jnp.argsort(token_order).astype(jnp.int32)
        return (attended_values.reshape(TOKENS, HEAD_SIZE)[inverse],
                attended_tangent_sum.reshape(TOKENS, HEAD_SIZE)[inverse])

    head_out, head_tan = lax.map(one_head, (routes.T,) + stacked)
    attended_values = head_out.transpose(1, 0, 2).reshape(TOKENS, HEADS * HEAD_SIZE)
    attended_tangent_sum = head_tan.transpose(1, 0, 2).reshape(TOKENS, HEADS * HEAD_SIZE)
    output = jnp.dot(attended_values, out_weight, preferred_element_type=jnp.float32).astype(jnp.bfloat16)
    output_tan = jnp.dot(attended_tangent_sum, out_weight, preferred_element_type=jnp.float32).astype(jnp.bfloat16)
    return (output, output_tan)
```

```python
import jax
import jax.numpy as jnp
from jax import lax
from jax.sharding import PartitionSpec as P

HEAD_SIZE = 128
CLUSTER = 256


def cluster_attend(q, k, v, dq, dk, dv, pos):
    scaling_multiplier = HEAD_SIZE ** (-0.5)
    logit_scores = (
        jnp.einsum("qe,ke->qk", q, k, preferred_element_type=jnp.float32) * scaling_multiplier
    )
    score_tangent_values = (
        jnp.einsum("qe,ke->qk", dq, k, preferred_element_type=jnp.float32)
        + jnp.einsum("qe,ke->qk", q, dk, preferred_element_type=jnp.float32)
    ) * scaling_multiplier
    visible = pos[None, :] <= pos[:, None]
    masked = jnp.where(visible, logit_scores, -jnp.inf)
    top_score = jnp.max(masked, axis=-1, keepdims=True)
    expo = jnp.where(visible, jnp.exp(masked - top_score), 0.0)
    attn_probs = expo / jnp.sum(expo, axis=-1, keepdims=True)
    probs_half = attn_probs.astype(jnp.bfloat16)
    attended_values = jnp.einsum(
        "qk,ke->qe", probs_half, v, preferred_element_type=jnp.float32
    ).astype(jnp.bfloat16)
    tangent_probs = attn_probs * (
        score_tangent_values - jnp.sum(attn_probs * score_tangent_values, axis=-1, keepdims=True)
    )
    tangent_half = tangent_probs.astype(jnp.bfloat16)
    attended_tangent_sum = (
        jnp.einsum("qk,ke->qe", tangent_half, v, preferred_element_type=jnp.float32)
        + jnp.einsum("qk,ke->qe", probs_half, dv, preferred_element_type=jnp.float32)
    ).astype(jnp.bfloat16)
    return attended_values, attended_tangent_sum


def body(query_rows, key_rows, value_rows, query_tan, key_tan, value_tan, routes, out_weight):
    tok_dev = routes.shape[0]
    heads_here = routes.shape[1]
    n_seq = lax.axis_size("seq")
    n_ten = lax.axis_size("tensor")
    inputs = (query_rows, key_rows, value_rows, query_tan, key_tan, value_tan)
    n_in = len(inputs)

    w_cols = lax.all_to_all(out_weight, "tensor", split_axis=1, concat_axis=0, tiled=True)

    rank = jnp.sum(
        (routes[None, :, :] < routes[:, None, :]).astype(jnp.int32), axis=1
    )
    slots = lax.broadcasted_iota(jnp.int32, (tok_dev, tok_dev), 0)
    perm = jnp.stack(
        [(rank[None, :, h] == slots).astype(jnp.bfloat16) for h in range(heads_here)]
    )

    local_pos = lax.broadcasted_iota(jnp.int32, (tok_dev, HEAD_SIZE), 0).astype(jnp.bfloat16)
    per_head = jnp.stack(
        [
            jnp.concatenate(
                [m[:, h * HEAD_SIZE:(h + 1) * HEAD_SIZE] for m in inputs] + [local_pos], axis=1
            )
            for h in range(heads_here)
        ]
    )
    sorted_rows = jnp.einsum(
        "hki,hif->khf", perm, per_head, preferred_element_type=jnp.float32
    ).astype(jnp.bfloat16)
    arrived = lax.all_to_all(sorted_rows, "seq", split_axis=0, concat_axis=0, tiled=True)

    per_src = tok_dev // n_seq
    src = lax.broadcasted_iota(jnp.int32, (tok_dev,), 0) // per_src
    outs = []
    for h in range(heads_here):
        cols = [arrived[:, h, i * HEAD_SIZE:(i + 1) * HEAD_SIZE] for i in range(n_in)]
        pos = src * tok_dev + arrived[:, h, n_in * HEAD_SIZE].astype(jnp.int32)
        a, at = cluster_attend(*cols, pos)
        outs.append(jnp.concatenate([a, at], axis=1))
    back = jnp.stack(outs, axis=1)
    returned = lax.all_to_all(back, "seq", split_axis=0, concat_axis=0, tiled=True)

    restored = jnp.einsum(
        "hki,khf->ihf", perm, returned, preferred_element_type=jnp.float32
    ).astype(jnp.bfloat16)
    restored = restored.reshape(tok_dev, heads_here, 2, HEAD_SIZE)
    local = jnp.transpose(restored, (2, 0, 1, 3)).reshape(2, tok_dev, heads_here * HEAD_SIZE)

    gathered = lax.all_gather(local, "tensor", axis=0, tiled=False)
    w_blocks = w_cols.reshape(n_ten, heads_here * HEAD_SIZE, w_cols.shape[1])
    projected = jnp.einsum(
        "poic,pcd->oid", gathered, w_blocks, preferred_element_type=jnp.float32
    )
    return (projected[0].astype(jnp.bfloat16), projected[1].astype(jnp.bfloat16))


def solution(mesh):
    return jax.shard_map(
        body,
        mesh=mesh,
        in_specs=(
            P("seq", "tensor"),
            P("seq", "tensor"),
            P("seq", "tensor"),
            P("seq", "tensor"),
            P("seq", "tensor"),
            P("seq", "tensor"),
            P("seq", "tensor"),
            P("tensor", None),
        ),
        out_specs=(P("seq", "tensor"), P("seq", "tensor")),
        check_vma=False,
    )
```

```python
import jax
import jax.numpy as jnp
from jax import lax
from jax.sharding import PartitionSpec as P

HEAD_SIZE = 128
CLUSTER = 256


def cluster_attend(q, k, v, dq, dk, dv, pos):
    scaling_multiplier = HEAD_SIZE ** (-0.5)
    logit_scores = (
        jnp.einsum("qe,ke->qk", q, k, preferred_element_type=jnp.float32) * scaling_multiplier
    )
    score_tangent_values = (
        jnp.einsum("qe,ke->qk", dq, k, preferred_element_type=jnp.float32)
        + jnp.einsum("qe,ke->qk", q, dk, preferred_element_type=jnp.float32)
    ) * scaling_multiplier
    visible = pos[None, :] <= pos[:, None]
    masked = jnp.where(visible, logit_scores, -jnp.inf)
    top_score = jnp.max(masked, axis=-1, keepdims=True)
    expo = jnp.where(visible, jnp.exp(masked - top_score), 0.0)
    attn_probs = expo / jnp.sum(expo, axis=-1, keepdims=True)
    probs_half = attn_probs.astype(jnp.bfloat16)
    attended_values = jnp.einsum(
        "qk,ke->qe", probs_half, v, preferred_element_type=jnp.float32
    ).astype(jnp.bfloat16)
    tangent_probs = attn_probs * (
        score_tangent_values - jnp.sum(attn_probs * score_tangent_values, axis=-1, keepdims=True)
    )
    tangent_half = tangent_probs.astype(jnp.bfloat16)
    attended_tangent_sum = (
        jnp.einsum("qk,ke->qe", tangent_half, v, preferred_element_type=jnp.float32)
        + jnp.einsum("qk,ke->qe", probs_half, dv, preferred_element_type=jnp.float32)
    ).astype(jnp.bfloat16)
    return attended_values, attended_tangent_sum


def body(query_rows, key_rows, value_rows, query_tan, key_tan, value_tan, routes, out_weight):
    tok_dev = routes.shape[0]
    heads_here = routes.shape[1]
    n_seq = lax.axis_size("seq")
    n_ten = lax.axis_size("tensor")
    inputs = (query_rows, key_rows, value_rows, query_tan, key_tan, value_tan)
    n_in = len(inputs)

    t_idx = lax.axis_index("tensor")
    blk = out_weight.shape[0]
    recv = [lax.dynamic_slice_in_dim(out_weight, t_idx * blk, blk, axis=1)]
    for k in range(1, n_ten):
        piece = lax.dynamic_slice_in_dim(out_weight, ((t_idx + k) % n_ten) * blk, blk, axis=1)
        recv.append(
            lax.ppermute(piece, "tensor", perm=[(i, (i + k) % n_ten) for i in range(n_ten)])
        )
    doubled = jnp.stack(recv[::-1] + recv[::-1])
    w_blocks = lax.dynamic_slice_in_dim(doubled, n_ten - 1 - t_idx, n_ten, axis=0)

    rank = jnp.sum(
        (routes[None, :, :] < routes[:, None, :]).astype(jnp.int32), axis=1
    )
    slots = lax.broadcasted_iota(jnp.int32, (tok_dev, tok_dev), 0)
    perm = jnp.stack(
        [(rank[None, :, h] == slots).astype(jnp.bfloat16) for h in range(heads_here)]
    )

    local_pos = lax.broadcasted_iota(jnp.int32, (tok_dev, HEAD_SIZE), 0).astype(jnp.bfloat16)
    per_head = jnp.stack(
        [
            jnp.concatenate(
                [m[:, h * HEAD_SIZE:(h + 1) * HEAD_SIZE] for m in inputs] + [local_pos], axis=1
            )
            for h in range(heads_here)
        ]
    )
    width = per_head.shape[2]
    sorted_rows = jnp.concatenate(
        [
            jnp.dot(perm[h], per_head[h], preferred_element_type=jnp.float32).astype(jnp.bfloat16)
            for h in range(heads_here)
        ],
        axis=1,
    )
    arrived = lax.all_to_all(sorted_rows, "seq", split_axis=0, concat_axis=0, tiled=True)

    per_src = tok_dev // n_seq
    src = lax.broadcasted_iota(jnp.int32, (tok_dev,), 0) // per_src
    outs = []
    for h in range(heads_here):
        base = h * width
        cols = [arrived[:, base + i * HEAD_SIZE:base + (i + 1) * HEAD_SIZE] for i in range(n_in)]
        pos = src * tok_dev + arrived[:, base + n_in * HEAD_SIZE].astype(jnp.int32)
        a, at = cluster_attend(*cols, pos)
        outs.append(jnp.concatenate([a, at], axis=1))
    back = jnp.concatenate(outs, axis=1)
    back, w_blocks = lax.optimization_barrier((back, w_blocks))
    returned = lax.all_to_all(back, "seq", split_axis=0, concat_axis=0, tiled=True)

    restored = [
        jnp.dot(
            perm[h].T,
            returned[:, h * 2 * HEAD_SIZE:(h + 1) * 2 * HEAD_SIZE],
            preferred_element_type=jnp.float32,
        ).astype(jnp.bfloat16)
        for h in range(heads_here)
    ]
    local = jnp.stack(
        [
            jnp.concatenate([r[:, o * HEAD_SIZE:(o + 1) * HEAD_SIZE] for r in restored], axis=1)
            for o in range(2)
        ]
    )

    gathered = lax.all_gather(local, "tensor", axis=0, tiled=False)
    projected = jnp.einsum(
        "poic,pcd->oid", gathered, w_blocks, preferred_element_type=jnp.float32
    )
    return (projected[0].astype(jnp.bfloat16), projected[1].astype(jnp.bfloat16))


def solution(mesh):
    return jax.shard_map(
        body,
        mesh=mesh,
        in_specs=(
            P("seq", "tensor"),
            P("seq", "tensor"),
            P("seq", "tensor"),
            P("seq", "tensor"),
            P("seq", "tensor"),
            P("seq", "tensor"),
            P("seq", "tensor"),
            P("tensor", None),
        ),
        out_specs=(P("seq", "tensor"), P("seq", "tensor")),
        check_vma=False,
    )
```

```python
import jax
import jax.numpy as jnp
from jax import lax
from jax.sharding import Mesh, PartitionSpec as P

HEAD_SIZE = 128
CLUSTER = 256


def cluster_attend(q, k, v, dq, dk, dv, pos):
    scaling_multiplier = HEAD_SIZE ** (-0.5)
    logit_scores = (
        jnp.einsum("qe,ke->qk", q, k, preferred_element_type=jnp.float32) * scaling_multiplier
    )
    score_tangent_values = (
        jnp.einsum("qe,ke->qk", dq, k, preferred_element_type=jnp.float32)
        + jnp.einsum("qe,ke->qk", q, dk, preferred_element_type=jnp.float32)
    ) * scaling_multiplier
    visible = pos[None, :] <= pos[:, None]
    masked = jnp.where(visible, logit_scores, -jnp.inf)
    top_score = jnp.max(masked, axis=-1, keepdims=True)
    expo = jnp.where(visible, jnp.exp(masked - top_score), 0.0)
    attn_probs = expo / jnp.sum(expo, axis=-1, keepdims=True)
    probs_half = attn_probs.astype(jnp.bfloat16)
    attended_values = jnp.einsum(
        "qk,ke->qe", probs_half, v, preferred_element_type=jnp.float32
    ).astype(jnp.bfloat16)
    tangent_probs = attn_probs * (
        score_tangent_values - jnp.sum(attn_probs * score_tangent_values, axis=-1, keepdims=True)
    )
    tangent_half = tangent_probs.astype(jnp.bfloat16)
    attended_tangent_sum = (
        jnp.einsum("qk,ke->qe", tangent_half, v, preferred_element_type=jnp.float32)
        + jnp.einsum("qk,ke->qe", probs_half, dv, preferred_element_type=jnp.float32)
    ).astype(jnp.bfloat16)
    return attended_values, attended_tangent_sum


def body(query_rows, key_rows, value_rows, query_tan, key_tan, value_tan, routes, out_weight):
    tok_dev = routes.shape[0]
    heads_here = routes.shape[1]
    n_seq = lax.axis_size("seq")
    inputs = (query_rows, key_rows, value_rows, query_tan, key_tan, value_tan)
    n_in = len(inputs)

    zh = lax.axis_index("zh")
    n_g = lax.axis_size("yc")
    blk = out_weight.shape[0]
    send_w = jnp.concatenate(
        [
            jnp.concatenate(
                [out_weight[:, j * blk:(j + 1) * blk], out_weight[:, (n_g + j) * blk:(n_g + j + 1) * blk]],
                axis=1,
            )
            for j in range(n_g)
        ],
        axis=0,
    )
    w_blocks = lax.all_to_all(send_w, "yc", split_axis=0, concat_axis=0, tiled=True).reshape(
        n_g, blk, 2 * blk
    )

    rank = jnp.sum(
        (routes[None, :, :] < routes[:, None, :]).astype(jnp.int32), axis=1
    )
    slots = lax.broadcasted_iota(jnp.int32, (tok_dev, tok_dev), 0)
    perm = jnp.stack(
        [(rank[None, :, h] == slots).astype(jnp.bfloat16) for h in range(heads_here)]
    )

    local_pos = lax.broadcasted_iota(jnp.int32, (tok_dev, HEAD_SIZE), 0).astype(jnp.bfloat16)
    per_head = jnp.stack(
        [
            jnp.concatenate(
                [m[:, h * HEAD_SIZE:(h + 1) * HEAD_SIZE] for m in inputs] + [local_pos], axis=1
            )
            for h in range(heads_here)
        ]
    )
    width = per_head.shape[2]
    sorted_rows = jnp.concatenate(
        [
            jnp.dot(perm[h], per_head[h], preferred_element_type=jnp.float32).astype(jnp.bfloat16)
            for h in range(heads_here)
        ],
        axis=1,
    )
    arrived = lax.all_to_all(sorted_rows, "seq", split_axis=0, concat_axis=0, tiled=True)

    per_src = tok_dev // n_seq
    src = lax.broadcasted_iota(jnp.int32, (tok_dev,), 0) // per_src
    outs = []
    for h in range(heads_here):
        base = h * width
        cols = [arrived[:, base + i * HEAD_SIZE:base + (i + 1) * HEAD_SIZE] for i in range(n_in)]
        pos = src * tok_dev + arrived[:, base + n_in * HEAD_SIZE].astype(jnp.int32)
        a, at = cluster_attend(*cols, pos)
        outs.append(jnp.concatenate([a, at], axis=1))
    back = jnp.concatenate(outs, axis=1)
    back, w_blocks = lax.optimization_barrier((back, w_blocks))
    returned = lax.all_to_all(back, "seq", split_axis=0, concat_axis=0, tiled=True)

    restored = [
        jnp.dot(
            perm[h].T,
            returned[:, h * 2 * HEAD_SIZE:(h + 1) * 2 * HEAD_SIZE],
            preferred_element_type=jnp.float32,
        ).astype(jnp.bfloat16)
        for h in range(heads_here)
    ]
    local = jnp.stack(
        [
            jnp.concatenate([r[:, o * HEAD_SIZE:(o + 1) * HEAD_SIZE] for r in restored], axis=1)
            for o in range(2)
        ]
    )

    gathered = lax.all_gather(local, "yc", axis=0, tiled=False)
    projected = jnp.einsum(
        "poic,pcd->oid", gathered, w_blocks, preferred_element_type=jnp.float32
    )
    mine = lax.dynamic_slice_in_dim(projected, zh * blk, blk, axis=2)
    theirs = lax.dynamic_slice_in_dim(projected, (1 - zh) * blk, blk, axis=2)
    other_half = lax.ppermute(theirs, "zh", perm=[(0, 1), (1, 0)])
    summed = mine + other_half
    return (summed[0].astype(jnp.bfloat16), summed[1].astype(jnp.bfloat16))


def solution(mesh):
    n_seq, n_ten = mesh.devices.shape
    split = Mesh(mesh.devices.reshape(n_seq, 2, n_ten // 2), ("seq", "zh", "yc"))
    rows = P("seq", ("zh", "yc"))
    return jax.shard_map(
        body,
        mesh=split,
        in_specs=(rows, rows, rows, rows, rows, rows, rows, P(("zh", "yc"), None)),
        out_specs=(rows, rows),
        check_vma=False,
    )
```

```python
import jax
import jax.numpy as jnp
from jax import lax
from jax.sharding import Mesh, PartitionSpec as P

HEAD_SIZE = 128
CLUSTER = 256


def cluster_attend(q, k, v, dq, dk, dv, pos):
    scaling_multiplier = HEAD_SIZE ** (-0.5)
    logit_scores = (
        jnp.einsum("qe,ke->qk", q, k, preferred_element_type=jnp.float32) * scaling_multiplier
    )
    score_tangent_values = (
        jnp.einsum("qe,ke->qk", dq, k, preferred_element_type=jnp.float32)
        + jnp.einsum("qe,ke->qk", q, dk, preferred_element_type=jnp.float32)
    ) * scaling_multiplier
    visible = pos[None, :] <= pos[:, None]
    masked = jnp.where(visible, logit_scores, -jnp.inf)
    top_score = jnp.max(masked, axis=-1, keepdims=True)
    expo = jnp.where(visible, jnp.exp(masked - top_score), 0.0)
    attn_probs = expo / jnp.sum(expo, axis=-1, keepdims=True)
    probs_half = attn_probs.astype(jnp.bfloat16)
    attended_values = jnp.einsum(
        "qk,ke->qe", probs_half, v, preferred_element_type=jnp.float32
    ).astype(jnp.bfloat16)
    tangent_probs = attn_probs * (
        score_tangent_values - jnp.sum(attn_probs * score_tangent_values, axis=-1, keepdims=True)
    )
    tangent_half = tangent_probs.astype(jnp.bfloat16)
    attended_tangent_sum = (
        jnp.einsum("qk,ke->qe", tangent_half, v, preferred_element_type=jnp.float32)
        + jnp.einsum("qk,ke->qe", probs_half, dv, preferred_element_type=jnp.float32)
    ).astype(jnp.bfloat16)
    return attended_values, attended_tangent_sum


def body(query_rows, key_rows, value_rows, query_tan, key_tan, value_tan, routes, out_weight):
    tok_dev = routes.shape[0]
    heads_here = routes.shape[1]
    n_seq = lax.axis_size("seq")
    inputs = (query_rows, key_rows, value_rows, query_tan, key_tan, value_tan)
    n_in = len(inputs)

    zh = lax.axis_index("zh")
    n_g = lax.axis_size("yc")
    blk = out_weight.shape[0]
    send_w = jnp.concatenate(
        [
            jnp.concatenate(
                [out_weight[:, j * blk:(j + 1) * blk], out_weight[:, (n_g + j) * blk:(n_g + j + 1) * blk]],
                axis=1,
            )
            for j in range(n_g)
        ],
        axis=0,
    )
    w_blocks = lax.all_to_all(send_w, "yc", split_axis=0, concat_axis=0, tiled=True).reshape(
        n_g, blk, 2 * blk
    )

    rank = jnp.sum(
        (routes[None, :, :] < routes[:, None, :]).astype(jnp.int32), axis=1
    )
    slots = lax.broadcasted_iota(jnp.int32, (tok_dev, tok_dev), 0)
    perm = jnp.stack(
        [(rank[None, :, h] == slots).astype(jnp.bfloat16) for h in range(heads_here)]
    )

    local_pos = lax.broadcasted_iota(jnp.int32, (tok_dev, HEAD_SIZE), 0).astype(jnp.bfloat16)
    per_head = jnp.stack(
        [
            jnp.concatenate(
                [m[:, h * HEAD_SIZE:(h + 1) * HEAD_SIZE] for m in inputs] + [local_pos], axis=1
            )
            for h in range(heads_here)
        ]
    )
    width = per_head.shape[2]
    sorted_rows = jnp.concatenate(
        [
            jnp.dot(perm[h], per_head[h], preferred_element_type=jnp.float32).astype(jnp.bfloat16)
            for h in range(heads_here)
        ],
        axis=1,
    )
    arrived = lax.all_to_all(sorted_rows, "seq", split_axis=0, concat_axis=0, tiled=True)

    per_src = tok_dev // n_seq
    src = lax.broadcasted_iota(jnp.int32, (tok_dev,), 0) // per_src
    outs = []
    for h in range(heads_here):
        base = h * width
        cols = [arrived[:, base + i * HEAD_SIZE:base + (i + 1) * HEAD_SIZE] for i in range(n_in)]
        pos = src * tok_dev + arrived[:, base + n_in * HEAD_SIZE].astype(jnp.int32)
        a, at = cluster_attend(*cols, pos)
        outs.append(jnp.concatenate([a, at], axis=1))
    back = jnp.concatenate(outs, axis=1)
    back, w_blocks = lax.optimization_barrier((back, w_blocks))
    returned = lax.all_to_all(back, "seq", split_axis=0, concat_axis=0, tiled=True)

    restored = [
        jnp.dot(
            perm[h].T,
            returned[:, h * 2 * HEAD_SIZE:(h + 1) * 2 * HEAD_SIZE],
            preferred_element_type=jnp.float32,
        ).astype(jnp.bfloat16)
        for h in range(heads_here)
    ]
    local = jnp.stack(
        [
            jnp.concatenate([r[:, o * HEAD_SIZE:(o + 1) * HEAD_SIZE] for r in restored], axis=1)
            for o in range(2)
        ]
    )

    gathered = lax.all_gather(local, "yc", axis=0, tiled=False)
    projected = jnp.einsum(
        "poic,pcd->oid", gathered, w_blocks, preferred_element_type=jnp.float32
    )
    mine = lax.dynamic_slice_in_dim(projected, zh * blk, blk, axis=2)
    theirs = lax.dynamic_slice_in_dim(projected, (1 - zh) * blk, blk, axis=2)
    other_half = lax.ppermute(theirs.astype(jnp.bfloat16), "zh", perm=[(0, 1), (1, 0)])
    summed = mine + other_half.astype(jnp.float32)
    return (summed[0].astype(jnp.bfloat16), summed[1].astype(jnp.bfloat16))


def solution(mesh):
    n_seq, n_ten = mesh.devices.shape
    split = Mesh(mesh.devices.reshape(n_seq, 2, n_ten // 2), ("seq", "zh", "yc"))
    rows = P("seq", ("zh", "yc"))
    return jax.shard_map(
        body,
        mesh=split,
        in_specs=(rows, rows, rows, rows, rows, rows, rows, P(("zh", "yc"), None)),
        out_specs=(rows, rows),
        check_vma=False,
    )
```

```python
import jax
import jax.numpy as jnp
from jax import lax
from jax.sharding import Mesh, PartitionSpec as P

HEAD_SIZE = 128
CLUSTER = 256


def cluster_attend(q, k, v, dq, dk, dv, pos):
    scaling_multiplier = HEAD_SIZE ** (-0.5)
    logit_scores = (
        jnp.einsum("qe,ke->qk", q, k, preferred_element_type=jnp.float32) * scaling_multiplier
    )
    score_tangent_values = (
        jnp.einsum("qe,ke->qk", dq, k, preferred_element_type=jnp.float32)
        + jnp.einsum("qe,ke->qk", q, dk, preferred_element_type=jnp.float32)
    ) * scaling_multiplier
    visible = pos[None, :] <= pos[:, None]
    masked = jnp.where(visible, logit_scores, -jnp.inf)
    top_score = jnp.max(masked, axis=-1, keepdims=True)
    expo = jnp.where(visible, jnp.exp(masked - top_score), 0.0)
    attn_probs = expo / jnp.sum(expo, axis=-1, keepdims=True)
    probs_half = attn_probs.astype(jnp.bfloat16)
    attended_values = jnp.einsum(
        "qk,ke->qe", probs_half, v, preferred_element_type=jnp.float32
    ).astype(jnp.bfloat16)
    tangent_probs = attn_probs * (
        score_tangent_values - jnp.sum(attn_probs * score_tangent_values, axis=-1, keepdims=True)
    )
    tangent_half = tangent_probs.astype(jnp.bfloat16)
    attended_tangent_sum = (
        jnp.einsum("qk,ke->qe", tangent_half, v, preferred_element_type=jnp.float32)
        + jnp.einsum("qk,ke->qe", probs_half, dv, preferred_element_type=jnp.float32)
    ).astype(jnp.bfloat16)
    return attended_values, attended_tangent_sum


def body(query_rows, key_rows, value_rows, query_tan, key_tan, value_tan, routes, out_weight):
    tok_dev = routes.shape[0]
    heads_here = routes.shape[1]
    n_seq = lax.axis_size("seq")
    inputs = (query_rows, key_rows, value_rows, query_tan, key_tan, value_tan)
    n_in = len(inputs)

    zh = lax.axis_index("zh")
    n_g = lax.axis_size("yc")
    blk = out_weight.shape[0]
    j_idx = lax.axis_index("yc")

    def cols_for(j):
        return jnp.concatenate(
            [
                lax.dynamic_slice_in_dim(out_weight, j * blk, blk, axis=1),
                lax.dynamic_slice_in_dim(out_weight, (n_g + j) * blk, blk, axis=1),
            ],
            axis=1,
        )

    recv = [cols_for(j_idx)]
    for k in range(1, n_g):
        recv.append(
            lax.ppermute(
                cols_for((j_idx + k) % n_g), "yc", perm=[(i, (i + k) % n_g) for i in range(n_g)]
            )
        )
    doubled = jnp.stack(recv[::-1] + recv[::-1])
    w_blocks = lax.dynamic_slice_in_dim(doubled, n_g - 1 - j_idx, n_g, axis=0)

    rank = jnp.sum(
        (routes[None, :, :] < routes[:, None, :]).astype(jnp.int32), axis=1
    )
    slots = lax.broadcasted_iota(jnp.int32, (tok_dev, tok_dev), 0)
    perm = jnp.stack(
        [(rank[None, :, h] == slots).astype(jnp.bfloat16) for h in range(heads_here)]
    )

    local_pos = lax.broadcasted_iota(jnp.int32, (tok_dev, HEAD_SIZE), 0).astype(jnp.bfloat16)
    per_head = jnp.stack(
        [
            jnp.concatenate(
                [m[:, h * HEAD_SIZE:(h + 1) * HEAD_SIZE] for m in inputs] + [local_pos], axis=1
            )
            for h in range(heads_here)
        ]
    )
    width = per_head.shape[2]
    sorted_rows = jnp.concatenate(
        [
            jnp.dot(perm[h], per_head[h], preferred_element_type=jnp.float32).astype(jnp.bfloat16)
            for h in range(heads_here)
        ],
        axis=1,
    )
    arrived = lax.all_to_all(sorted_rows, "seq", split_axis=0, concat_axis=0, tiled=True)

    per_src = tok_dev // n_seq
    src = lax.broadcasted_iota(jnp.int32, (tok_dev,), 0) // per_src
    outs = []
    for h in range(heads_here):
        base = h * width
        cols = [arrived[:, base + i * HEAD_SIZE:base + (i + 1) * HEAD_SIZE] for i in range(n_in)]
        pos = src * tok_dev + arrived[:, base + n_in * HEAD_SIZE].astype(jnp.int32)
        a, at = cluster_attend(*cols, pos)
        outs.append(jnp.concatenate([a, at], axis=1))
    back = jnp.concatenate(outs, axis=1)
    back, w_blocks = lax.optimization_barrier((back, w_blocks))
    back, w_blocks = lax.optimization_barrier((back, w_blocks))
    returned = lax.all_to_all(back, "seq", split_axis=0, concat_axis=0, tiled=True)

    restored = [
        jnp.dot(
            perm[h].T,
            returned[:, h * 2 * HEAD_SIZE:(h + 1) * 2 * HEAD_SIZE],
            preferred_element_type=jnp.float32,
        ).astype(jnp.bfloat16)
        for h in range(heads_here)
    ]
    local = jnp.stack(
        [
            jnp.concatenate([r[:, o * HEAD_SIZE:(o + 1) * HEAD_SIZE] for r in restored], axis=1)
            for o in range(2)
        ]
    )

    gathered = lax.all_gather(local, "yc", axis=0, tiled=False)
    projected = jnp.einsum(
        "poic,pcd->oid", gathered, w_blocks, preferred_element_type=jnp.float32
    )
    mine = lax.dynamic_slice_in_dim(projected, zh * blk, blk, axis=2)
    theirs = lax.dynamic_slice_in_dim(projected, (1 - zh) * blk, blk, axis=2)
    other_half = lax.ppermute(theirs.astype(jnp.bfloat16), "zh", perm=[(0, 1), (1, 0)])
    summed = mine + other_half.astype(jnp.float32)
    return (summed[0].astype(jnp.bfloat16), summed[1].astype(jnp.bfloat16))


def solution(mesh):
    n_seq, n_ten = mesh.devices.shape
    split = Mesh(mesh.devices.reshape(n_seq, 2, n_ten // 2), ("seq", "zh", "yc"))
    rows = P("seq", ("zh", "yc"))
    return jax.shard_map(
        body,
        mesh=split,
        in_specs=(rows, rows, rows, rows, rows, rows, rows, P(("zh", "yc"), None)),
        out_specs=(rows, rows),
        check_vma=False,
    )
```

```python
import jax
import jax.numpy as jnp
from jax import lax
from jax.sharding import Mesh, PartitionSpec as P

HEAD_SIZE = 128
CLUSTER = 256


def cluster_attend(q, k, v, dq, dk, dv, pos):
    scaling_multiplier = HEAD_SIZE ** (-0.5)
    logit_scores = (
        jnp.einsum("qe,ke->qk", q, k, preferred_element_type=jnp.float32) * scaling_multiplier
    )
    score_tangent_values = (
        jnp.einsum("qe,ke->qk", dq, k, preferred_element_type=jnp.float32)
        + jnp.einsum("qe,ke->qk", q, dk, preferred_element_type=jnp.float32)
    ) * scaling_multiplier
    visible = pos[None, :] <= pos[:, None]
    masked = jnp.where(visible, logit_scores, -jnp.inf)
    top_score = jnp.max(masked, axis=-1, keepdims=True)
    expo = jnp.where(visible, jnp.exp(masked - top_score), 0.0)
    attn_probs = expo / jnp.sum(expo, axis=-1, keepdims=True)
    probs_half = attn_probs.astype(jnp.bfloat16)
    attended_values = jnp.einsum(
        "qk,ke->qe", probs_half, v, preferred_element_type=jnp.float32
    ).astype(jnp.bfloat16)
    tangent_probs = attn_probs * (
        score_tangent_values - jnp.sum(attn_probs * score_tangent_values, axis=-1, keepdims=True)
    )
    tangent_half = tangent_probs.astype(jnp.bfloat16)
    attended_tangent_sum = (
        jnp.einsum("qk,ke->qe", tangent_half, v, preferred_element_type=jnp.float32)
        + jnp.einsum("qk,ke->qe", probs_half, dv, preferred_element_type=jnp.float32)
    ).astype(jnp.bfloat16)
    return attended_values, attended_tangent_sum


def body(query_rows, key_rows, value_rows, query_tan, key_tan, value_tan, routes, out_weight):
    tok_dev = routes.shape[0]
    heads_here = routes.shape[1]
    n_seq = lax.axis_size("seq")
    inputs = (query_rows, key_rows, value_rows, query_tan, key_tan, value_tan)
    n_in = len(inputs)

    zh = lax.axis_index("zh")
    n_g = lax.axis_size("yc")
    blk = out_weight.shape[0]
    j_idx = lax.axis_index("yc")

    def cols_for(j):
        return jnp.concatenate(
            [
                lax.dynamic_slice_in_dim(out_weight, j * blk, blk, axis=1),
                lax.dynamic_slice_in_dim(out_weight, (n_g + j) * blk, blk, axis=1),
            ],
            axis=1,
        )

    recv = [cols_for(j_idx)]
    for k in range(1, n_g):
        recv.append(
            lax.ppermute(
                cols_for((j_idx + k) % n_g), "yc", perm=[(i, (i + k) % n_g) for i in range(n_g)]
            )
        )
    doubled = jnp.stack(recv[::-1] + recv[::-1])
    w_blocks = lax.dynamic_slice_in_dim(doubled, n_g - 1 - j_idx, n_g, axis=0)

    token = lax.broadcasted_iota(jnp.int32, routes.shape, 0)
    key = (routes // CLUSTER) * tok_dev + token
    rank = jnp.sum((key[None, :, :] < key[:, None, :]).astype(jnp.int32), axis=1)
    slots = lax.broadcasted_iota(jnp.int32, (tok_dev, tok_dev), 0)
    perm = jnp.stack(
        [(rank[None, :, h] == slots).astype(jnp.bfloat16) for h in range(heads_here)]
    )

    per_head = jnp.stack(
        [
            jnp.concatenate([m[:, h * HEAD_SIZE:(h + 1) * HEAD_SIZE] for m in inputs], axis=1)
            for h in range(heads_here)
        ]
    )
    width = per_head.shape[2]
    sorted_rows = jnp.concatenate(
        [
            jnp.dot(perm[h], per_head[h], preferred_element_type=jnp.float32).astype(jnp.bfloat16)
            for h in range(heads_here)
        ],
        axis=1,
    )
    arrived = lax.all_to_all(sorted_rows, "seq", split_axis=0, concat_axis=0, tiled=True)

    pos = lax.broadcasted_iota(jnp.int32, (tok_dev,), 0)
    outs = []
    for h in range(heads_here):
        base = h * width
        cols = [arrived[:, base + i * HEAD_SIZE:base + (i + 1) * HEAD_SIZE] for i in range(n_in)]
        a, at = cluster_attend(*cols, pos)
        outs.append(jnp.concatenate([a, at], axis=1))
    back = jnp.concatenate(outs, axis=1)
    back, w_blocks = lax.optimization_barrier((back, w_blocks))
    back, w_blocks = lax.optimization_barrier((back, w_blocks))
    returned = lax.all_to_all(back, "seq", split_axis=0, concat_axis=0, tiled=True)

    restored = [
        jnp.dot(
            perm[h].T,
            returned[:, h * 2 * HEAD_SIZE:(h + 1) * 2 * HEAD_SIZE],
            preferred_element_type=jnp.float32,
        ).astype(jnp.bfloat16)
        for h in range(heads_here)
    ]
    local = jnp.stack(
        [
            jnp.concatenate([r[:, o * HEAD_SIZE:(o + 1) * HEAD_SIZE] for r in restored], axis=1)
            for o in range(2)
        ]
    )

    gathered = lax.all_gather(local, "yc", axis=0, tiled=False)
    projected = jnp.einsum(
        "poic,pcd->oid", gathered, w_blocks, preferred_element_type=jnp.float32
    )
    mine = lax.dynamic_slice_in_dim(projected, zh * blk, blk, axis=2)
    theirs = lax.dynamic_slice_in_dim(projected, (1 - zh) * blk, blk, axis=2)
    other_half = lax.ppermute(theirs.astype(jnp.bfloat16), "zh", perm=[(0, 1), (1, 0)])
    summed = mine + other_half.astype(jnp.float32)
    return (summed[0].astype(jnp.bfloat16), summed[1].astype(jnp.bfloat16))


def solution(mesh):
    n_seq, n_ten = mesh.devices.shape
    split = Mesh(mesh.devices.reshape(n_seq, 2, n_ten // 2), ("seq", "zh", "yc"))
    rows = P("seq", ("zh", "yc"))
    return jax.shard_map(
        body,
        mesh=split,
        in_specs=(rows, rows, rows, rows, rows, rows, rows, P(("zh", "yc"), None)),
        out_specs=(rows, rows),
        check_vma=False,
    )
```

```python
import jax
import jax.numpy as jnp
from jax import lax
from jax.sharding import Mesh, PartitionSpec as P

HEAD_SIZE = 128
CLUSTER = 256


def cluster_attend(q, k, v, dq, dk, dv, pos):
    scaling_multiplier = HEAD_SIZE ** (-0.5)
    logit_scores = (
        jnp.einsum("qe,ke->qk", q, k, preferred_element_type=jnp.float32) * scaling_multiplier
    )
    score_tangent_values = (
        jnp.einsum("qe,ke->qk", dq, k, preferred_element_type=jnp.float32)
        + jnp.einsum("qe,ke->qk", q, dk, preferred_element_type=jnp.float32)
    ) * scaling_multiplier
    visible = pos[None, :] <= pos[:, None]
    masked = jnp.where(visible, logit_scores, -jnp.inf)
    top_score = jnp.max(masked, axis=-1, keepdims=True)
    expo = jnp.where(visible, jnp.exp(masked - top_score), 0.0)
    attn_probs = expo / jnp.sum(expo, axis=-1, keepdims=True)
    probs_half = attn_probs.astype(jnp.bfloat16)
    attended_values = jnp.einsum(
        "qk,ke->qe", probs_half, v, preferred_element_type=jnp.float32
    ).astype(jnp.bfloat16)
    tangent_probs = attn_probs * (
        score_tangent_values - jnp.sum(attn_probs * score_tangent_values, axis=-1, keepdims=True)
    )
    tangent_half = tangent_probs.astype(jnp.bfloat16)
    attended_tangent_sum = (
        jnp.einsum("qk,ke->qe", tangent_half, v, preferred_element_type=jnp.float32)
        + jnp.einsum("qk,ke->qe", probs_half, dv, preferred_element_type=jnp.float32)
    ).astype(jnp.bfloat16)
    return attended_values, attended_tangent_sum


def body(query_rows, key_rows, value_rows, query_tan, key_tan, value_tan, routes, out_weight):
    tok_dev = routes.shape[0]
    heads_here = routes.shape[1]
    n_seq = lax.axis_size("seq")
    inputs = (query_rows, key_rows, value_rows, query_tan, key_tan, value_tan)
    n_in = len(inputs)

    zh = lax.axis_index("zh")
    n_g = lax.axis_size("yc")
    blk = out_weight.shape[0]
    j_idx = lax.axis_index("yc")

    def cols_for(j):
        return jnp.concatenate(
            [
                lax.dynamic_slice_in_dim(out_weight, j * blk, blk, axis=1),
                lax.dynamic_slice_in_dim(out_weight, (n_g + j) * blk, blk, axis=1),
            ],
            axis=1,
        )

    recv = [cols_for(j_idx)]
    for k in range(1, n_g):
        recv.append(
            lax.ppermute(
                cols_for((j_idx + k) % n_g), "yc", perm=[(i, (i + k) % n_g) for i in range(n_g)]
            )
        )
    doubled = jnp.stack(recv[::-1] + recv[::-1])
    w_blocks = lax.dynamic_slice_in_dim(doubled, n_g - 1 - j_idx, n_g, axis=0)

    token = lax.broadcasted_iota(jnp.int32, routes.shape, 0)
    key = (routes // CLUSTER) * tok_dev + token
    rank = jnp.sum((key[None, :, :] < key[:, None, :]).astype(jnp.int32), axis=1)
    slots = lax.broadcasted_iota(jnp.int32, (tok_dev, tok_dev), 0)
    perm = jnp.stack(
        [(rank[None, :, h] == slots).astype(jnp.bfloat16) for h in range(heads_here)]
    )

    per_head = jnp.stack(
        [
            jnp.concatenate([m[:, h * HEAD_SIZE:(h + 1) * HEAD_SIZE] for m in inputs], axis=1)
            for h in range(heads_here)
        ]
    )
    width = per_head.shape[2]
    sorted_rows = jnp.concatenate(
        [
            jnp.dot(perm[h], per_head[h], preferred_element_type=jnp.float32).astype(jnp.bfloat16)
            for h in range(heads_here)
        ],
        axis=1,
    )
    arrived = lax.all_to_all(sorted_rows, "seq", split_axis=0, concat_axis=0, tiled=True)

    pos = lax.broadcasted_iota(jnp.int32, (tok_dev,), 0)
    outs = []
    for h in range(heads_here):
        base = h * width
        cols = [arrived[:, base + i * HEAD_SIZE:base + (i + 1) * HEAD_SIZE] for i in range(n_in)]
        a, at = cluster_attend(*cols, pos)
        outs.append((a, at))
    backs = [jnp.concatenate([o[which] for o in outs], axis=1) for which in range(2)]
    backs, w_blocks = lax.optimization_barrier((backs, w_blocks))
    results = []
    for back in backs:
        returned = lax.all_to_all(back, "seq", split_axis=0, concat_axis=0, tiled=True)
        local = jnp.concatenate(
            [
                jnp.dot(
                    perm[h].T,
                    returned[:, h * HEAD_SIZE:(h + 1) * HEAD_SIZE],
                    preferred_element_type=jnp.float32,
                ).astype(jnp.bfloat16)
                for h in range(heads_here)
            ],
            axis=1,
        )
        gathered = lax.all_gather(local, "yc", axis=0, tiled=False)
        projected = jnp.einsum(
            "pic,pcd->id", gathered, w_blocks, preferred_element_type=jnp.float32
        )
        mine = lax.dynamic_slice_in_dim(projected, zh * blk, blk, axis=1)
        theirs = lax.dynamic_slice_in_dim(projected, (1 - zh) * blk, blk, axis=1)
        other_half = lax.ppermute(theirs.astype(jnp.bfloat16), "zh", perm=[(0, 1), (1, 0)])
        results.append((mine + other_half.astype(jnp.float32)).astype(jnp.bfloat16))
    return tuple(results)


def solution(mesh):
    n_seq, n_ten = mesh.devices.shape
    split = Mesh(mesh.devices.reshape(n_seq, 2, n_ten // 2), ("seq", "zh", "yc"))
    rows = P("seq", ("zh", "yc"))
    return jax.shard_map(
        body,
        mesh=split,
        in_specs=(rows, rows, rows, rows, rows, rows, rows, P(("zh", "yc"), None)),
        out_specs=(rows, rows),
        check_vma=False,
    )
```

```python
import jax
import jax.numpy as jnp
from jax import lax
from jax.sharding import Mesh, PartitionSpec as P

HEAD_SIZE = 128
CLUSTER = 256


def cluster_attend(q, k, v, dq, dk, dv, pos):
    scaling_multiplier = HEAD_SIZE ** (-0.5)
    logit_scores = (
        jnp.einsum("qe,ke->qk", q, k, preferred_element_type=jnp.float32) * scaling_multiplier
    )
    score_tangent_values = (
        jnp.einsum("qe,ke->qk", dq, k, preferred_element_type=jnp.float32)
        + jnp.einsum("qe,ke->qk", q, dk, preferred_element_type=jnp.float32)
    ) * scaling_multiplier
    visible = pos[None, :] <= pos[:, None]
    masked = jnp.where(visible, logit_scores, -jnp.inf)
    top_score = jnp.max(masked, axis=-1, keepdims=True)
    expo = jnp.where(visible, jnp.exp(masked - top_score), 0.0)
    attn_probs = expo / jnp.sum(expo, axis=-1, keepdims=True)
    probs_half = attn_probs.astype(jnp.bfloat16)
    attended_values = jnp.einsum(
        "qk,ke->qe", probs_half, v, preferred_element_type=jnp.float32
    ).astype(jnp.bfloat16)
    tangent_probs = attn_probs * (
        score_tangent_values - jnp.sum(attn_probs * score_tangent_values, axis=-1, keepdims=True)
    )
    tangent_half = tangent_probs.astype(jnp.bfloat16)
    attended_tangent_sum = (
        jnp.einsum("qk,ke->qe", tangent_half, v, preferred_element_type=jnp.float32)
        + jnp.einsum("qk,ke->qe", probs_half, dv, preferred_element_type=jnp.float32)
    ).astype(jnp.bfloat16)
    return attended_values, attended_tangent_sum


def body(query_rows, key_rows, value_rows, query_tan, key_tan, value_tan, routes, out_weight):
    tok_dev = routes.shape[0]
    heads_here = routes.shape[1]
    n_seq = lax.axis_size("seq")
    inputs = (query_rows, key_rows, value_rows, query_tan, key_tan, value_tan)
    n_in = len(inputs)

    zh = lax.axis_index("zh")
    n_g = lax.axis_size("yc")
    blk = out_weight.shape[0]
    j_idx = lax.axis_index("yc")

    def cols_for(j):
        return jnp.concatenate(
            [
                lax.dynamic_slice_in_dim(out_weight, j * blk, blk, axis=1),
                lax.dynamic_slice_in_dim(out_weight, (n_g + j) * blk, blk, axis=1),
            ],
            axis=1,
        )

    recv = [cols_for(j_idx)]
    for k in range(1, n_g):
        recv.append(
            lax.ppermute(
                cols_for((j_idx + k) % n_g), "yc", perm=[(i, (i + k) % n_g) for i in range(n_g)]
            )
        )
    w_blocks = jnp.stack(recv)

    token = lax.broadcasted_iota(jnp.int32, routes.shape, 0)
    key = (routes // CLUSTER) * tok_dev + token
    rank = jnp.sum((key[None, :, :] < key[:, None, :]).astype(jnp.int32), axis=1)
    slots = lax.broadcasted_iota(jnp.int32, (tok_dev, tok_dev), 0)
    perm = jnp.stack(
        [(rank[None, :, h] == slots).astype(jnp.bfloat16) for h in range(heads_here)]
    )

    per_head = jnp.stack(
        [
            jnp.concatenate([m[:, h * HEAD_SIZE:(h + 1) * HEAD_SIZE] for m in inputs], axis=1)
            for h in range(heads_here)
        ]
    )
    width = per_head.shape[2]
    sorted_rows = jnp.concatenate(
        [
            jnp.dot(perm[h], per_head[h], preferred_element_type=jnp.float32).astype(jnp.bfloat16)
            for h in range(heads_here)
        ],
        axis=1,
    )
    arrived = lax.all_to_all(sorted_rows, "seq", split_axis=0, concat_axis=0, tiled=True)

    pos = lax.broadcasted_iota(jnp.int32, (tok_dev,), 0)
    outs = []
    for h in range(heads_here):
        base = h * width
        cols = [arrived[:, base + i * HEAD_SIZE:base + (i + 1) * HEAD_SIZE] for i in range(n_in)]
        a, at = cluster_attend(*cols, pos)
        outs.append(jnp.concatenate([a, at], axis=1))
    back = jnp.concatenate(outs, axis=1)
    back, w_blocks = lax.optimization_barrier((back, w_blocks))
    back, w_blocks = lax.optimization_barrier((back, w_blocks))
    returned = lax.all_to_all(back, "seq", split_axis=0, concat_axis=0, tiled=True)

    restored = [
        jnp.dot(
            perm[h].T,
            returned[:, h * 2 * HEAD_SIZE:(h + 1) * 2 * HEAD_SIZE],
            preferred_element_type=jnp.float32,
        ).astype(jnp.bfloat16)
        for h in range(heads_here)
    ]
    local = jnp.stack(
        [
            jnp.concatenate([r[:, o * HEAD_SIZE:(o + 1) * HEAD_SIZE] for r in restored], axis=1)
            for o in range(2)
        ]
    )

    flat = jnp.concatenate([local[0], local[1]], axis=1)
    shifted = [flat] + [
        lax.ppermute(flat, "yc", perm=[(i, (i + k) % n_g) for i in range(n_g)])
        for k in range(1, n_g)
    ]
    gathered = jnp.stack(shifted).reshape(n_g, tok_dev, 2, heads_here * HEAD_SIZE)
    projected = jnp.einsum(
        "kioc,kcd->oid", gathered, w_blocks, preferred_element_type=jnp.float32
    )
    mine = lax.dynamic_slice_in_dim(projected, zh * blk, blk, axis=2)
    theirs = lax.dynamic_slice_in_dim(projected, (1 - zh) * blk, blk, axis=2)
    other_half = lax.ppermute(theirs.astype(jnp.bfloat16), "zh", perm=[(0, 1), (1, 0)])
    summed = mine + other_half.astype(jnp.float32)
    return (summed[0].astype(jnp.bfloat16), summed[1].astype(jnp.bfloat16))


def solution(mesh):
    n_seq, n_ten = mesh.devices.shape
    split = Mesh(mesh.devices.reshape(n_seq, 2, n_ten // 2), ("seq", "zh", "yc"))
    rows = P("seq", ("zh", "yc"))
    return jax.shard_map(
        body,
        mesh=split,
        in_specs=(rows, rows, rows, rows, rows, rows, rows, P(("zh", "yc"), None)),
        out_specs=(rows, rows),
        check_vma=False,
    )
```

```python
import jax
import jax.numpy as jnp
from jax import lax
from jax.sharding import Mesh, PartitionSpec as P

HEAD_SIZE = 128
CLUSTER = 256


def cluster_attend(q, k, v, dq, dk, dv, pos):
    scaling_multiplier = HEAD_SIZE ** (-0.5)
    logit_scores = (
        jnp.einsum("qe,ke->qk", q, k, preferred_element_type=jnp.float32) * scaling_multiplier
    )
    score_tangent_values = (
        jnp.einsum("qe,ke->qk", dq, k, preferred_element_type=jnp.float32)
        + jnp.einsum("qe,ke->qk", q, dk, preferred_element_type=jnp.float32)
    ) * scaling_multiplier
    visible = pos[None, :] <= pos[:, None]
    masked = jnp.where(visible, logit_scores, -jnp.inf)
    top_score = jnp.max(masked, axis=-1, keepdims=True)
    expo = jnp.where(visible, jnp.exp(masked - top_score), 0.0)
    attn_probs = expo / jnp.sum(expo, axis=-1, keepdims=True)
    probs_half = attn_probs.astype(jnp.bfloat16)
    attended_values = jnp.einsum(
        "qk,ke->qe", probs_half, v, preferred_element_type=jnp.float32
    ).astype(jnp.bfloat16)
    tangent_probs = attn_probs * (
        score_tangent_values - jnp.sum(attn_probs * score_tangent_values, axis=-1, keepdims=True)
    )
    tangent_half = tangent_probs.astype(jnp.bfloat16)
    attended_tangent_sum = (
        jnp.einsum("qk,ke->qe", tangent_half, v, preferred_element_type=jnp.float32)
        + jnp.einsum("qk,ke->qe", probs_half, dv, preferred_element_type=jnp.float32)
    ).astype(jnp.bfloat16)
    return attended_values, attended_tangent_sum


def body(query_rows, key_rows, value_rows, query_tan, key_tan, value_tan, routes, out_weight):
    tok_dev = routes.shape[0]
    heads_here = routes.shape[1]
    n_seq = lax.axis_size("seq")
    inputs = (query_rows, key_rows, value_rows, query_tan, key_tan, value_tan)
    n_in = len(inputs)

    zh = lax.axis_index("zh")
    n_g = lax.axis_size("yc")
    blk = out_weight.shape[0]
    j_idx = lax.axis_index("yc")

    def cols_for(j):
        return jnp.concatenate(
            [
                lax.dynamic_slice_in_dim(out_weight, j * blk, blk, axis=1),
                lax.dynamic_slice_in_dim(out_weight, (n_g + j) * blk, blk, axis=1),
            ],
            axis=1,
        )

    n_y = n_g // 2
    w_same = [cols_for(j_idx)]
    for m in range(1, n_y):
        w_same.append(
            lax.ppermute(
                cols_for((j_idx + 2 * m) % n_g),
                "yc",
                perm=[(i, (i + 2 * m) % n_g) for i in range(n_g)],
            )
        )
    w_other = []
    for m in range(n_y):
        dest = jnp.bitwise_xor((j_idx + 2 * m) % n_g, 1)
        w_other.append(
            lax.ppermute(
                cols_for(dest), "yc", perm=[(i, ((i + 2 * m) % n_g) ^ 1) for i in range(n_g)]
            )
        )
    w_blocks = (jnp.stack(w_same), jnp.stack(w_other))

    token = lax.broadcasted_iota(jnp.int32, routes.shape, 0)
    key = (routes // CLUSTER) * tok_dev + token
    rank = jnp.sum((key[None, :, :] < key[:, None, :]).astype(jnp.int32), axis=1)
    slots = lax.broadcasted_iota(jnp.int32, (tok_dev, tok_dev), 0)
    perm = jnp.stack(
        [(rank[None, :, h] == slots).astype(jnp.bfloat16) for h in range(heads_here)]
    )

    per_head = jnp.stack(
        [
            jnp.concatenate([m[:, h * HEAD_SIZE:(h + 1) * HEAD_SIZE] for m in inputs], axis=1)
            for h in range(heads_here)
        ]
    )
    width = per_head.shape[2]
    sorted_rows = jnp.concatenate(
        [
            jnp.dot(perm[h], per_head[h], preferred_element_type=jnp.float32).astype(jnp.bfloat16)
            for h in range(heads_here)
        ],
        axis=1,
    )
    arrived = lax.all_to_all(sorted_rows, "seq", split_axis=0, concat_axis=0, tiled=True)

    pos = lax.broadcasted_iota(jnp.int32, (tok_dev,), 0)
    outs = []
    for h in range(heads_here):
        base = h * width
        cols = [arrived[:, base + i * HEAD_SIZE:base + (i + 1) * HEAD_SIZE] for i in range(n_in)]
        a, at = cluster_attend(*cols, pos)
        outs.append(jnp.concatenate([a, at], axis=1))
    back = jnp.concatenate(outs, axis=1)
    back, w_blocks = lax.optimization_barrier((back, w_blocks))
    back, w_blocks = lax.optimization_barrier((back, w_blocks))
    returned = lax.all_to_all(back, "seq", split_axis=0, concat_axis=0, tiled=True)

    restored = [
        jnp.dot(
            perm[h].T,
            returned[:, h * 2 * HEAD_SIZE:(h + 1) * 2 * HEAD_SIZE],
            preferred_element_type=jnp.float32,
        ).astype(jnp.bfloat16)
        for h in range(heads_here)
    ]
    local = jnp.stack(
        [
            jnp.concatenate([r[:, o * HEAD_SIZE:(o + 1) * HEAD_SIZE] for r in restored], axis=1)
            for o in range(2)
        ]
    )

    flat = jnp.concatenate([local[0], local[1]], axis=1)
    same = jnp.stack(
        [flat]
        + [
            lax.ppermute(flat, "yc", perm=[(i, (i + 2 * m) % n_g) for i in range(n_g)])
            for m in range(1, n_y)
        ]
    )
    other = lax.ppermute(same, "yc", perm=[(i, i ^ 1) for i in range(n_g)])
    shape4 = (n_y, tok_dev, 2, heads_here * HEAD_SIZE)
    projected = jnp.einsum(
        "kioc,kcd->oid", same.reshape(shape4), w_blocks[0], preferred_element_type=jnp.float32
    ) + jnp.einsum(
        "kioc,kcd->oid", other.reshape(shape4), w_blocks[1], preferred_element_type=jnp.float32
    )
    mine = lax.dynamic_slice_in_dim(projected, zh * blk, blk, axis=2)
    theirs = lax.dynamic_slice_in_dim(projected, (1 - zh) * blk, blk, axis=2)
    other_half = lax.ppermute(theirs.astype(jnp.bfloat16), "zh", perm=[(0, 1), (1, 0)])
    summed = mine + other_half.astype(jnp.float32)
    return (summed[0].astype(jnp.bfloat16), summed[1].astype(jnp.bfloat16))


def solution(mesh):
    n_seq, n_ten = mesh.devices.shape
    split = Mesh(mesh.devices.reshape(n_seq, 2, n_ten // 2), ("seq", "zh", "yc"))
    rows = P("seq", ("zh", "yc"))
    return jax.shard_map(
        body,
        mesh=split,
        in_specs=(rows, rows, rows, rows, rows, rows, rows, P(("zh", "yc"), None)),
        out_specs=(rows, rows),
        check_vma=False,
    )
```

```python
import jax
import jax.numpy as jnp
from jax import lax
from jax.sharding import Mesh, PartitionSpec as P

HEAD_SIZE = 128
CLUSTER = 256


def cluster_attend(q, k, v, dq, dk, dv, pos):
    scaling_multiplier = HEAD_SIZE ** (-0.5)
    logit_scores = (
        jnp.einsum("qe,ke->qk", q, k, preferred_element_type=jnp.float32) * scaling_multiplier
    )
    score_tangent_values = (
        jnp.einsum("qe,ke->qk", dq, k, preferred_element_type=jnp.float32)
        + jnp.einsum("qe,ke->qk", q, dk, preferred_element_type=jnp.float32)
    ) * scaling_multiplier
    visible = pos[None, :] <= pos[:, None]
    masked = jnp.where(visible, logit_scores, -jnp.inf)
    top_score = jnp.max(masked, axis=-1, keepdims=True)
    expo = jnp.where(visible, jnp.exp(masked - top_score), 0.0)
    attn_probs = expo / jnp.sum(expo, axis=-1, keepdims=True)
    probs_half = attn_probs.astype(jnp.bfloat16)
    attended_values = jnp.einsum(
        "qk,ke->qe", probs_half, v, preferred_element_type=jnp.float32
    ).astype(jnp.bfloat16)
    tangent_probs = attn_probs * (
        score_tangent_values - jnp.sum(attn_probs * score_tangent_values, axis=-1, keepdims=True)
    )
    tangent_half = tangent_probs.astype(jnp.bfloat16)
    attended_tangent_sum = (
        jnp.einsum("qk,ke->qe", tangent_half, v, preferred_element_type=jnp.float32)
        + jnp.einsum("qk,ke->qe", probs_half, dv, preferred_element_type=jnp.float32)
    ).astype(jnp.bfloat16)
    return attended_values, attended_tangent_sum


def body(query_rows, key_rows, value_rows, query_tan, key_tan, value_tan, routes, out_weight):
    tok_dev = routes.shape[0]
    heads_here = routes.shape[1]
    n_seq = lax.axis_size("seq")
    inputs = (query_rows, key_rows, value_rows, query_tan, key_tan, value_tan)
    n_in = len(inputs)

    zh = lax.axis_index("zh")
    n_g = lax.axis_size("yc")
    blk = out_weight.shape[0]
    j_idx = lax.axis_index("yc")

    def cols_for(j):
        return jnp.concatenate(
            [
                lax.dynamic_slice_in_dim(out_weight, (zh * n_g + j) * blk, blk, axis=1),
                lax.dynamic_slice_in_dim(out_weight, ((1 - zh) * n_g + j) * blk, blk, axis=1),
            ],
            axis=1,
        )

    n_y = n_g // 2
    w_same = [cols_for(j_idx)]
    for m in range(1, n_y):
        w_same.append(
            lax.ppermute(
                cols_for((j_idx + 2 * m) % n_g),
                "yc",
                perm=[(i, (i + 2 * m) % n_g) for i in range(n_g)],
            )
        )
    w_other = []
    for m in range(n_y):
        dest = jnp.bitwise_xor((j_idx + 2 * m) % n_g, 1)
        w_other.append(
            lax.ppermute(
                cols_for(dest), "yc", perm=[(i, ((i + 2 * m) % n_g) ^ 1) for i in range(n_g)]
            )
        )
    w_blocks = (jnp.stack(w_same), jnp.stack(w_other))

    token = lax.broadcasted_iota(jnp.int32, routes.shape, 0)
    key = (routes // CLUSTER) * tok_dev + token
    rank = jnp.sum((key[None, :, :] < key[:, None, :]).astype(jnp.int32), axis=1)
    slots = lax.broadcasted_iota(jnp.int32, (tok_dev, tok_dev), 0)
    perm = jnp.stack(
        [(rank[None, :, h] == slots).astype(jnp.bfloat16) for h in range(heads_here)]
    )

    rows_in = jnp.concatenate(inputs, axis=1)
    col_head = (
        lax.broadcasted_iota(jnp.int32, (1, rows_in.shape[1]), 1) // HEAD_SIZE
    ) % heads_here
    sorted_rows = jnp.zeros(rows_in.shape, jnp.float32)
    for h in range(heads_here):
        sorted_rows = jnp.where(
            col_head == h,
            jnp.dot(perm[h], rows_in, preferred_element_type=jnp.float32),
            sorted_rows,
        )
    sorted_rows = sorted_rows.astype(jnp.bfloat16)
    arrived = lax.all_to_all(sorted_rows, "seq", split_axis=0, concat_axis=0, tiled=True)

    pos = lax.broadcasted_iota(jnp.int32, (tok_dev,), 0)
    outs = []
    for h in range(heads_here):
        cols = [
            arrived[:, (i * heads_here + h) * HEAD_SIZE:(i * heads_here + h + 1) * HEAD_SIZE]
            for i in range(n_in)
        ]
        a, at = cluster_attend(*cols, pos)
        outs.append(jnp.concatenate([a, at], axis=1))
    back = jnp.concatenate(outs, axis=1)
    back, w_blocks = lax.optimization_barrier((back, w_blocks))
    back, w_blocks = lax.optimization_barrier((back, w_blocks))
    returned = lax.all_to_all(back, "seq", split_axis=0, concat_axis=0, tiled=True)

    restored = [
        jnp.dot(
            perm[h].T,
            returned[:, h * 2 * HEAD_SIZE:(h + 1) * 2 * HEAD_SIZE],
            preferred_element_type=jnp.float32,
        ).astype(jnp.bfloat16)
        for h in range(heads_here)
    ]
    local = jnp.stack(
        [
            jnp.concatenate([r[:, o * HEAD_SIZE:(o + 1) * HEAD_SIZE] for r in restored], axis=1)
            for o in range(2)
        ]
    )

    flat = jnp.concatenate([local[0], local[1]], axis=1)
    same = jnp.stack(
        [flat]
        + [
            lax.ppermute(flat, "yc", perm=[(i, (i + 2 * m) % n_g) for i in range(n_g)])
            for m in range(1, n_y)
        ]
    )
    other = lax.ppermute(same, "yc", perm=[(i, i ^ 1) for i in range(n_g)])
    shape4 = (n_y, tok_dev, 2, heads_here * HEAD_SIZE)

    def project(cols):
        part = slice(cols * blk, (cols + 1) * blk)
        return jnp.einsum(
            "kioc,kcd->oid", same.reshape(shape4), w_blocks[0][:, :, part],
            preferred_element_type=jnp.float32,
        ) + jnp.einsum(
            "kioc,kcd->oid", other.reshape(shape4), w_blocks[1][:, :, part],
            preferred_element_type=jnp.float32,
        )

    theirs = project(1)
    other_half = lax.ppermute(theirs.astype(jnp.bfloat16), "zh", perm=[(0, 1), (1, 0)])
    mine = project(0)
    return tuple(
        (mine[o] + other_half[o].astype(jnp.float32)).astype(jnp.bfloat16) for o in range(2)
    )


def solution(mesh):
    n_seq, n_ten = mesh.devices.shape
    split = Mesh(mesh.devices.reshape(n_seq, 2, n_ten // 2), ("seq", "zh", "yc"))
    rows = P("seq", ("zh", "yc"))
    return jax.shard_map(
        body,
        mesh=split,
        in_specs=(rows, rows, rows, rows, rows, rows, rows, P(("zh", "yc"), None)),
        out_specs=(rows, rows),
        check_vma=False,
    )
```

```python
import jax
import jax.numpy as jnp
from jax import lax
from jax.sharding import Mesh, PartitionSpec as P

HEAD_SIZE = 128
CLUSTER = 256


def cluster_attend(q, k, v, dq, dk, dv, pos):
    scaling_multiplier = HEAD_SIZE ** (-0.5)
    logit_scores = (
        jnp.einsum("qe,ke->qk", q, k, preferred_element_type=jnp.float32) * scaling_multiplier
    )
    score_tangent_values = (
        jnp.einsum("qe,ke->qk", dq, k, preferred_element_type=jnp.float32)
        + jnp.einsum("qe,ke->qk", q, dk, preferred_element_type=jnp.float32)
    ) * scaling_multiplier
    visible = pos[None, :] <= pos[:, None]
    masked = jnp.where(visible, logit_scores, -jnp.inf)
    top_score = jnp.max(masked, axis=-1, keepdims=True)
    expo = jnp.where(visible, jnp.exp(masked - top_score), 0.0)
    attn_probs = expo / jnp.sum(expo, axis=-1, keepdims=True)
    probs_half = attn_probs.astype(jnp.bfloat16)
    attended_values = jnp.einsum(
        "qk,ke->qe", probs_half, v, preferred_element_type=jnp.float32
    ).astype(jnp.bfloat16)
    tangent_probs = attn_probs * (
        score_tangent_values - jnp.sum(attn_probs * score_tangent_values, axis=-1, keepdims=True)
    )
    tangent_half = tangent_probs.astype(jnp.bfloat16)
    attended_tangent_sum = (
        jnp.einsum("qk,ke->qe", tangent_half, v, preferred_element_type=jnp.float32)
        + jnp.einsum("qk,ke->qe", probs_half, dv, preferred_element_type=jnp.float32)
    ).astype(jnp.bfloat16)
    return attended_values, attended_tangent_sum


def body(query_rows, key_rows, value_rows, query_tan, key_tan, value_tan, routes, out_weight):
    tok_dev = routes.shape[0]
    heads_here = routes.shape[1]
    n_seq = lax.axis_size("seq")
    inputs = (query_rows, key_rows, value_rows, query_tan, key_tan, value_tan)
    n_in = len(inputs)

    zh = lax.axis_index("zh")
    n_g = lax.axis_size("yc")
    blk = out_weight.shape[0]
    j_idx = lax.axis_index("yc")

    def cols_for(j):
        return jnp.concatenate(
            [
                lax.dynamic_slice_in_dim(out_weight, j * blk, blk, axis=1),
                lax.dynamic_slice_in_dim(out_weight, (n_g + j) * blk, blk, axis=1),
            ],
            axis=1,
        )

    n_y = n_g // 2
    def pair_cols(j):
        return jnp.concatenate([cols_for(j), cols_for(jnp.bitwise_xor(j, 1))], axis=1)

    w_pairs = [pair_cols(j_idx)]
    for m in range(1, n_y):
        w_pairs.append(
            lax.ppermute(
                pair_cols((j_idx + 2 * m) % n_g),
                "yc",
                perm=[(i, (i + 2 * m) % n_g) for i in range(n_g)],
            )
        )
    w_same = [p[:, :2 * blk] for p in w_pairs]
    w_other = lax.ppermute(
        jnp.stack([p[:, 2 * blk:] for p in w_pairs]), "yc", perm=[(i, i ^ 1) for i in range(n_g)]
    )
    w_blocks = (jnp.stack(w_same), w_other)

    token = lax.broadcasted_iota(jnp.int32, routes.shape, 0)
    key = (routes // CLUSTER) * tok_dev + token
    rank = jnp.sum((key[None, :, :] < key[:, None, :]).astype(jnp.int32), axis=1)
    slots = lax.broadcasted_iota(jnp.int32, (tok_dev, tok_dev), 0)
    perm = jnp.stack(
        [(rank[None, :, h] == slots).astype(jnp.bfloat16) for h in range(heads_here)]
    )

    per_head = jnp.stack(
        [
            jnp.concatenate([m[:, h * HEAD_SIZE:(h + 1) * HEAD_SIZE] for m in inputs], axis=1)
            for h in range(heads_here)
        ]
    )
    width = per_head.shape[2]
    sorted_rows = jnp.concatenate(
        [
            jnp.dot(perm[h], per_head[h], preferred_element_type=jnp.float32).astype(jnp.bfloat16)
            for h in range(heads_here)
        ],
        axis=1,
    )
    arrived = lax.all_to_all(sorted_rows, "seq", split_axis=0, concat_axis=0, tiled=True)

    pos = lax.broadcasted_iota(jnp.int32, (tok_dev,), 0)
    outs = []
    for h in range(heads_here):
        base = h * width
        cols = [arrived[:, base + i * HEAD_SIZE:base + (i + 1) * HEAD_SIZE] for i in range(n_in)]
        a, at = cluster_attend(*cols, pos)
        outs.append(jnp.concatenate([a, at], axis=1))
    back = jnp.concatenate(outs, axis=1)
    back, w_blocks = lax.optimization_barrier((back, w_blocks))
    back, w_blocks = lax.optimization_barrier((back, w_blocks))
    returned = lax.all_to_all(back, "seq", split_axis=0, concat_axis=0, tiled=True)

    restored = [
        jnp.dot(
            perm[h].T,
            returned[:, h * 2 * HEAD_SIZE:(h + 1) * 2 * HEAD_SIZE],
            preferred_element_type=jnp.float32,
        ).astype(jnp.bfloat16)
        for h in range(heads_here)
    ]
    local = jnp.stack(
        [
            jnp.concatenate([r[:, o * HEAD_SIZE:(o + 1) * HEAD_SIZE] for r in restored], axis=1)
            for o in range(2)
        ]
    )

    flat = jnp.concatenate([local[0], local[1]], axis=1)
    same = jnp.stack(
        [flat]
        + [
            lax.ppermute(flat, "yc", perm=[(i, (i + 2 * m) % n_g) for i in range(n_g)])
            for m in range(1, n_y)
        ]
    )
    other = lax.ppermute(same, "yc", perm=[(i, i ^ 1) for i in range(n_g)])
    shape4 = (n_y, tok_dev, 2, heads_here * HEAD_SIZE)
    projected = jnp.einsum(
        "kioc,kcd->oid", same.reshape(shape4), w_blocks[0], preferred_element_type=jnp.float32
    ) + jnp.einsum(
        "kioc,kcd->oid", other.reshape(shape4), w_blocks[1], preferred_element_type=jnp.float32
    )
    mine = lax.dynamic_slice_in_dim(projected, zh * blk, blk, axis=2)
    theirs = lax.dynamic_slice_in_dim(projected, (1 - zh) * blk, blk, axis=2)
    other_half = lax.ppermute(theirs.astype(jnp.bfloat16), "zh", perm=[(0, 1), (1, 0)])
    summed = mine + other_half.astype(jnp.float32)
    return (summed[0].astype(jnp.bfloat16), summed[1].astype(jnp.bfloat16))


def solution(mesh):
    n_seq, n_ten = mesh.devices.shape
    split = Mesh(mesh.devices.reshape(n_seq, 2, n_ten // 2), ("seq", "zh", "yc"))
    rows = P("seq", ("zh", "yc"))
    return jax.shard_map(
        body,
        mesh=split,
        in_specs=(rows, rows, rows, rows, rows, rows, rows, P(("zh", "yc"), None)),
        out_specs=(rows, rows),
        check_vma=False,
    )
```

```python
import jax
import jax.numpy as jnp
from jax import lax
from jax.sharding import Mesh, PartitionSpec as P

HEAD_SIZE = 128
CLUSTER = 256


def cluster_attend(q, k, v, dq, dk, dv, pos):
    scaling_multiplier = HEAD_SIZE ** (-0.5)
    logit_scores = (
        jnp.einsum("qe,ke->qk", q, k, preferred_element_type=jnp.float32) * scaling_multiplier
    )
    score_tangent_values = (
        jnp.einsum("qe,ke->qk", dq, k, preferred_element_type=jnp.float32)
        + jnp.einsum("qe,ke->qk", q, dk, preferred_element_type=jnp.float32)
    ) * scaling_multiplier
    visible = pos[None, :] <= pos[:, None]
    masked = jnp.where(visible, logit_scores, -jnp.inf)
    top_score = jnp.max(masked, axis=-1, keepdims=True)
    expo = jnp.where(visible, jnp.exp(masked - top_score), 0.0)
    attn_probs = expo / jnp.sum(expo, axis=-1, keepdims=True)
    probs_half = attn_probs.astype(jnp.bfloat16)
    attended_values = jnp.einsum(
        "qk,ke->qe", probs_half, v, preferred_element_type=jnp.float32
    ).astype(jnp.bfloat16)
    tangent_probs = attn_probs * (
        score_tangent_values - jnp.sum(attn_probs * score_tangent_values, axis=-1, keepdims=True)
    )
    tangent_half = tangent_probs.astype(jnp.bfloat16)
    attended_tangent_sum = (
        jnp.einsum("qk,ke->qe", tangent_half, v, preferred_element_type=jnp.float32)
        + jnp.einsum("qk,ke->qe", probs_half, dv, preferred_element_type=jnp.float32)
    ).astype(jnp.bfloat16)
    return attended_values, attended_tangent_sum


def body(query_rows, key_rows, value_rows, query_tan, key_tan, value_tan, routes, out_weight):
    tok_dev = routes.shape[0]
    heads_here = routes.shape[1]
    n_seq = lax.axis_size("seq")
    inputs = (query_rows, key_rows, value_rows, query_tan, key_tan, value_tan)
    n_in = len(inputs)

    zh = lax.axis_index("zh")
    n_g = lax.axis_size("yc")
    blk = out_weight.shape[0]
    j_idx = lax.axis_index("yc")

    def cols_for(j):
        return jnp.concatenate(
            [
                lax.dynamic_slice_in_dim(out_weight, j * blk, blk, axis=1),
                lax.dynamic_slice_in_dim(out_weight, (n_g + j) * blk, blk, axis=1),
            ],
            axis=1,
        )

    n_y = n_g // 2
    def pair_cols(j):
        return jnp.concatenate([cols_for(j), cols_for(jnp.bitwise_xor(j, 1))], axis=1)

    w_pairs = [pair_cols(j_idx)]
    for m in range(1, n_y):
        w_pairs.append(
            lax.ppermute(
                pair_cols((j_idx + 2 * m) % n_g),
                "yc",
                perm=[(i, (i + 2 * m) % n_g) for i in range(n_g)],
            )
        )
    w_same = [p[:, :2 * blk] for p in w_pairs]
    w_other = lax.ppermute(
        jnp.stack([p[:, 2 * blk:] for p in w_pairs]), "yc", perm=[(i, i ^ 1) for i in range(n_g)]
    )
    w_blocks = (jnp.stack(w_same), w_other)

    token = lax.broadcasted_iota(jnp.int32, routes.shape, 0)
    key = (routes // CLUSTER) * tok_dev + token
    rank = jnp.sum((key[None, :, :] < key[:, None, :]).astype(jnp.int32), axis=1)
    slots = lax.broadcasted_iota(jnp.int32, (tok_dev, tok_dev), 0)
    perm = jnp.stack(
        [(rank[None, :, h] == slots).astype(jnp.bfloat16) for h in range(heads_here)]
    )

    per_head = jnp.stack(
        [
            jnp.concatenate([m[:, h * HEAD_SIZE:(h + 1) * HEAD_SIZE] for m in inputs], axis=1)
            for h in range(heads_here)
        ]
    )
    width = per_head.shape[2]
    sorted_rows = jnp.concatenate(
        [
            jnp.dot(perm[h], per_head[h], preferred_element_type=jnp.float32).astype(jnp.bfloat16)
            for h in range(heads_here)
        ],
        axis=1,
    )
    arrived = lax.all_to_all(sorted_rows, "seq", split_axis=0, concat_axis=0, tiled=True)

    pos = lax.broadcasted_iota(jnp.int32, (tok_dev,), 0)
    outs = []
    for h in range(heads_here):
        base = h * width
        cols = [arrived[:, base + i * HEAD_SIZE:base + (i + 1) * HEAD_SIZE] for i in range(n_in)]
        a, at = cluster_attend(*cols, pos)
        outs.append(jnp.concatenate([a, at], axis=1))
    back = jnp.concatenate(outs, axis=1)
    returned = lax.all_to_all(back, "seq", split_axis=0, concat_axis=0, tiled=True)

    restored = [
        jnp.dot(
            perm[h].T,
            returned[:, h * 2 * HEAD_SIZE:(h + 1) * 2 * HEAD_SIZE],
            preferred_element_type=jnp.float32,
        ).astype(jnp.bfloat16)
        for h in range(heads_here)
    ]
    local = jnp.stack(
        [
            jnp.concatenate([r[:, o * HEAD_SIZE:(o + 1) * HEAD_SIZE] for r in restored], axis=1)
            for o in range(2)
        ]
    )

    flat = jnp.concatenate([local[0], local[1]], axis=1)
    same = jnp.stack(
        [flat]
        + [
            lax.ppermute(flat, "yc", perm=[(i, (i + 2 * m) % n_g) for i in range(n_g)])
            for m in range(1, n_y)
        ]
    )
    other = lax.ppermute(same, "yc", perm=[(i, i ^ 1) for i in range(n_g)])
    shape4 = (n_y, tok_dev, 2, heads_here * HEAD_SIZE)
    projected = jnp.einsum(
        "kioc,kcd->oid", same.reshape(shape4), w_blocks[0], preferred_element_type=jnp.float32
    ) + jnp.einsum(
        "kioc,kcd->oid", other.reshape(shape4), w_blocks[1], preferred_element_type=jnp.float32
    )
    mine = lax.dynamic_slice_in_dim(projected, zh * blk, blk, axis=2)
    theirs = lax.dynamic_slice_in_dim(projected, (1 - zh) * blk, blk, axis=2)
    other_half = lax.ppermute(theirs.astype(jnp.bfloat16), "zh", perm=[(0, 1), (1, 0)])
    summed = mine + other_half.astype(jnp.float32)
    return (summed[0].astype(jnp.bfloat16), summed[1].astype(jnp.bfloat16))


def solution(mesh):
    n_seq, n_ten = mesh.devices.shape
    split = Mesh(mesh.devices.reshape(n_seq, 2, n_ten // 2), ("seq", "zh", "yc"))
    rows = P("seq", ("zh", "yc"))
    return jax.shard_map(
        body,
        mesh=split,
        in_specs=(rows, rows, rows, rows, rows, rows, rows, P(("zh", "yc"), None)),
        out_specs=(rows, rows),
        check_vma=False,
    )
```

```python
import jax
import jax.numpy as jnp
from jax import lax
from jax.sharding import Mesh, PartitionSpec as P

HEAD_SIZE = 128
CLUSTER = 256


def cluster_attend(q, k, v, dq, dk, dv, pos):
    scaling_multiplier = HEAD_SIZE ** (-0.5)
    logit_scores = (
        jnp.einsum("qe,ke->qk", q, k, preferred_element_type=jnp.float32) * scaling_multiplier
    )
    score_tangent_values = (
        jnp.einsum("qe,ke->qk", dq, k, preferred_element_type=jnp.float32)
        + jnp.einsum("qe,ke->qk", q, dk, preferred_element_type=jnp.float32)
    ) * scaling_multiplier
    visible = pos[None, :] <= pos[:, None]
    masked = jnp.where(visible, logit_scores, -jnp.inf)
    top_score = jnp.max(masked, axis=-1, keepdims=True)
    expo = jnp.where(visible, jnp.exp(masked - top_score), 0.0)
    attn_probs = expo / jnp.sum(expo, axis=-1, keepdims=True)
    probs_half = attn_probs.astype(jnp.bfloat16)
    attended_values = jnp.einsum(
        "qk,ke->qe", probs_half, v, preferred_element_type=jnp.float32
    ).astype(jnp.bfloat16)
    tangent_probs = attn_probs * (
        score_tangent_values - jnp.sum(attn_probs * score_tangent_values, axis=-1, keepdims=True)
    )
    tangent_half = tangent_probs.astype(jnp.bfloat16)
    attended_tangent_sum = (
        jnp.einsum("qk,ke->qe", tangent_half, v, preferred_element_type=jnp.float32)
        + jnp.einsum("qk,ke->qe", probs_half, dv, preferred_element_type=jnp.float32)
    ).astype(jnp.bfloat16)
    return attended_values, attended_tangent_sum


def body(query_rows, key_rows, value_rows, query_tan, key_tan, value_tan, routes, out_weight):
    tok_dev = routes.shape[0]
    heads_here = routes.shape[1]
    n_seq = lax.axis_size("seq")
    inputs = (query_rows, key_rows, value_rows, query_tan, key_tan, value_tan)
    n_in = len(inputs)

    zh = lax.axis_index("zh")
    n_g = lax.axis_size("yc")
    blk = out_weight.shape[0]
    j_idx = lax.axis_index("yc")

    def cols_for(j):
        return jnp.concatenate(
            [
                lax.dynamic_slice_in_dim(out_weight, j * blk, blk, axis=1),
                lax.dynamic_slice_in_dim(out_weight, (n_g + j) * blk, blk, axis=1),
            ],
            axis=1,
        )

    n_y = n_g // 2
    def pair_cols(j):
        return jnp.concatenate([cols_for(j), cols_for(jnp.bitwise_xor(j, 1))], axis=1)

    w_pairs = [pair_cols(j_idx)]
    for m in range(1, n_y):
        w_pairs.append(
            lax.ppermute(
                pair_cols((j_idx + 2 * m) % n_g),
                "yc",
                perm=[(i, (i + 2 * m) % n_g) for i in range(n_g)],
            )
        )
    w_same = [p[:, :2 * blk] for p in w_pairs]
    w_other = lax.ppermute(
        jnp.stack([p[:, 2 * blk:] for p in w_pairs]), "yc", perm=[(i, i ^ 1) for i in range(n_g)]
    )
    w_blocks = (jnp.stack(w_same), w_other)

    token = lax.broadcasted_iota(jnp.int32, routes.shape, 0)
    key = (routes // CLUSTER) * tok_dev + token
    rank = jnp.sum((key[None, :, :] < key[:, None, :]).astype(jnp.int32), axis=1)
    slots = lax.broadcasted_iota(jnp.int32, (tok_dev, tok_dev), 0)
    perm = jnp.stack(
        [(rank[None, :, h] == slots).astype(jnp.bfloat16) for h in range(heads_here)]
    )

    per_head = jnp.stack(
        [
            jnp.concatenate([m[:, h * HEAD_SIZE:(h + 1) * HEAD_SIZE] for m in inputs], axis=1)
            for h in range(heads_here)
        ]
    )
    width = per_head.shape[2]
    sorted_rows = jnp.concatenate(
        [
            jnp.dot(perm[h], per_head[h], preferred_element_type=jnp.float32).astype(jnp.bfloat16)
            for h in range(heads_here)
        ],
        axis=1,
    )
    arrived = lax.all_to_all(sorted_rows, "seq", split_axis=0, concat_axis=0, tiled=True)

    pos = lax.broadcasted_iota(jnp.int32, (tok_dev,), 0)
    outs = []
    for h in range(heads_here):
        base = h * width
        cols = [arrived[:, base + i * HEAD_SIZE:base + (i + 1) * HEAD_SIZE] for i in range(n_in)]
        a, at = cluster_attend(*cols, pos)
        outs.append(jnp.concatenate([a, at], axis=1))
    back = jnp.concatenate(outs, axis=1)
    returned = lax.all_to_all(back, "seq", split_axis=0, concat_axis=0, tiled=True)

    restored = [
        jnp.dot(
            perm[h].T,
            returned[:, h * 2 * HEAD_SIZE:(h + 1) * 2 * HEAD_SIZE],
            preferred_element_type=jnp.float32,
        ).astype(jnp.bfloat16)
        for h in range(heads_here)
    ]
    local = jnp.stack(
        [
            jnp.concatenate([r[:, o * HEAD_SIZE:(o + 1) * HEAD_SIZE] for r in restored], axis=1)
            for o in range(2)
        ]
    )

    flat = jnp.concatenate([local[0], local[1]], axis=1)
    same = jnp.stack(
        [flat]
        + [
            lax.ppermute(flat, "yc", perm=[(i, (i + 2 * m) % n_g) for i in range(n_g)])
            for m in range(1, n_y)
        ]
    )
    other = lax.ppermute(same, "yc", perm=[(i, i ^ 1) for i in range(n_g)])
    shape4 = (n_y, tok_dev, 2, heads_here * HEAD_SIZE)

    def project(half):
        return sum(
            jnp.einsum(
                "kioc,kcd->oid",
                blocks.reshape(shape4),
                lax.dynamic_slice_in_dim(w, half * blk, blk, axis=2),
                preferred_element_type=jnp.float32,
            )
            for blocks, w in ((same, w_blocks[0]), (other, w_blocks[1]))
        )

    theirs = project(1 - zh)
    other_half = lax.ppermute(theirs.astype(jnp.bfloat16), "zh", perm=[(0, 1), (1, 0)])
    mine = project(zh)
    return tuple(
        (mine[o] + other_half[o].astype(jnp.float32)).astype(jnp.bfloat16) for o in range(2)
    )


def solution(mesh):
    n_seq, n_ten = mesh.devices.shape
    split = Mesh(mesh.devices.reshape(n_seq, 2, n_ten // 2), ("seq", "zh", "yc"))
    rows = P("seq", ("zh", "yc"))
    return jax.shard_map(
        body,
        mesh=split,
        in_specs=(rows, rows, rows, rows, rows, rows, rows, P(("zh", "yc"), None)),
        out_specs=(rows, rows),
        check_vma=False,
    )
```

```python
import jax
import jax.numpy as jnp
from jax import lax
from jax.sharding import Mesh, PartitionSpec as P

HEAD_SIZE = 128
CLUSTER = 256


def cluster_attend(q, k, v, dq, dk, dv, pos):
    scaling_multiplier = HEAD_SIZE ** (-0.5)
    logit_scores = (
        jnp.einsum("qe,ke->qk", q, k, preferred_element_type=jnp.float32) * scaling_multiplier
    )
    score_tangent_values = (
        jnp.einsum("qe,ke->qk", dq, k, preferred_element_type=jnp.float32)
        + jnp.einsum("qe,ke->qk", q, dk, preferred_element_type=jnp.float32)
    ) * scaling_multiplier
    visible = pos[None, :] <= pos[:, None]
    masked = jnp.where(visible, logit_scores, -jnp.inf)
    top_score = jnp.max(masked, axis=-1, keepdims=True)
    expo = jnp.where(visible, jnp.exp(masked - top_score), 0.0)
    attn_probs = expo / jnp.sum(expo, axis=-1, keepdims=True)
    probs_half = attn_probs.astype(jnp.bfloat16)
    attended_values = jnp.einsum(
        "qk,ke->qe", probs_half, v, preferred_element_type=jnp.float32
    ).astype(jnp.bfloat16)
    tangent_probs = attn_probs * (
        score_tangent_values - jnp.sum(attn_probs * score_tangent_values, axis=-1, keepdims=True)
    )
    tangent_half = tangent_probs.astype(jnp.bfloat16)
    attended_tangent_sum = (
        jnp.einsum("qk,ke->qe", tangent_half, v, preferred_element_type=jnp.float32)
        + jnp.einsum("qk,ke->qe", probs_half, dv, preferred_element_type=jnp.float32)
    ).astype(jnp.bfloat16)
    return attended_values, attended_tangent_sum


def body(query_rows, key_rows, value_rows, query_tan, key_tan, value_tan, routes, out_weight):
    tok_dev = routes.shape[0]
    heads_here = routes.shape[1]
    n_seq = lax.axis_size("seq")
    inputs = (query_rows, key_rows, value_rows, query_tan, key_tan, value_tan)
    n_in = len(inputs)

    zh = lax.axis_index("zh")
    n_g = lax.axis_size("yc")
    blk = out_weight.shape[0]
    j_idx = lax.axis_index("yc")

    def cols_for(j):
        return jnp.concatenate(
            [
                lax.dynamic_slice_in_dim(out_weight, j * blk, blk, axis=1),
                lax.dynamic_slice_in_dim(out_weight, (n_g + j) * blk, blk, axis=1),
            ],
            axis=1,
        )

    n_y = n_g // 2
    def pair_cols(j):
        return jnp.concatenate([cols_for(j), cols_for(jnp.bitwise_xor(j, 1))], axis=1)

    w_pairs = [pair_cols(j_idx)]
    for m in range(1, n_y):
        w_pairs.append(
            lax.ppermute(
                pair_cols((j_idx + 2 * m) % n_g),
                "yc",
                perm=[(i, (i + 2 * m) % n_g) for i in range(n_g)],
            )
        )
    w_same = [p[:, :2 * blk] for p in w_pairs]
    w_other = lax.ppermute(
        jnp.stack([p[:, 2 * blk:] for p in w_pairs]), "yc", perm=[(i, i ^ 1) for i in range(n_g)]
    )
    w_blocks = (jnp.stack(w_same), w_other)

    token = lax.broadcasted_iota(jnp.int32, routes.shape, 0)
    key = (routes // CLUSTER) * tok_dev + token
    rank = jnp.sum((key[None, :, :] < key[:, None, :]).astype(jnp.int32), axis=1)
    slots = lax.broadcasted_iota(jnp.int32, (tok_dev, tok_dev), 0)
    perm = jnp.stack(
        [(rank[None, :, h] == slots).astype(jnp.bfloat16) for h in range(heads_here)]
    )

    per_head = jnp.stack(
        [
            jnp.concatenate([m[:, h * HEAD_SIZE:(h + 1) * HEAD_SIZE] for m in inputs], axis=1)
            for h in range(heads_here)
        ]
    )
    width = per_head.shape[2]
    sorted_rows = jnp.concatenate(
        [
            jnp.dot(perm[h], per_head[h], preferred_element_type=jnp.float32).astype(jnp.bfloat16)
            for h in range(heads_here)
        ],
        axis=1,
    )
    arrived = lax.all_to_all(sorted_rows, "seq", split_axis=0, concat_axis=0, tiled=True)

    pos = lax.broadcasted_iota(jnp.int32, (tok_dev,), 0)
    outs = []
    for h in range(heads_here):
        base = h * width
        cols = [arrived[:, base + i * HEAD_SIZE:base + (i + 1) * HEAD_SIZE] for i in range(n_in)]
        a, at = cluster_attend(*cols, pos)
        outs.append(jnp.concatenate([a, at], axis=1))
    back = jnp.concatenate(outs, axis=1)
    returned = lax.all_to_all(back, "seq", split_axis=0, concat_axis=0, tiled=True)

    restored = [
        jnp.dot(
            perm[h].T,
            returned[:, h * 2 * HEAD_SIZE:(h + 1) * 2 * HEAD_SIZE],
            preferred_element_type=jnp.float32,
        ).astype(jnp.bfloat16)
        for h in range(heads_here)
    ]
    local = jnp.stack(
        [
            jnp.concatenate([r[:, o * HEAD_SIZE:(o + 1) * HEAD_SIZE] for r in restored], axis=1)
            for o in range(2)
        ]
    )

    flat = jnp.concatenate([local[0], local[1]], axis=1)
    same = [flat] + [
        lax.ppermute(flat, "yc", perm=[(i, (i + 2 * m) % n_g) for i in range(n_g)])
        for m in range(1, n_y)
    ]
    other = [lax.ppermute(b, "yc", perm=[(i, i ^ 1) for i in range(n_g)]) for b in same]
    shape3 = (tok_dev, 2, heads_here * HEAD_SIZE)
    projected = sum(
        jnp.einsum("ioc,cd->oid", b.reshape(shape3), w[m], preferred_element_type=jnp.float32)
        for blocks, w in ((same, w_blocks[0]), (other, w_blocks[1]))
        for m, b in enumerate(blocks)
    )
    mine = lax.dynamic_slice_in_dim(projected, zh * blk, blk, axis=2)
    theirs = lax.dynamic_slice_in_dim(projected, (1 - zh) * blk, blk, axis=2)
    other_half = lax.ppermute(theirs.astype(jnp.bfloat16), "zh", perm=[(0, 1), (1, 0)])
    summed = mine + other_half.astype(jnp.float32)
    return (summed[0].astype(jnp.bfloat16), summed[1].astype(jnp.bfloat16))


def solution(mesh):
    n_seq, n_ten = mesh.devices.shape
    split = Mesh(mesh.devices.reshape(n_seq, 2, n_ten // 2), ("seq", "zh", "yc"))
    rows = P("seq", ("zh", "yc"))
    return jax.shard_map(
        body,
        mesh=split,
        in_specs=(rows, rows, rows, rows, rows, rows, rows, P(("zh", "yc"), None)),
        out_specs=(rows, rows),
        check_vma=False,
    )
```

```python
import jax
import jax.numpy as jnp
from jax import lax
from jax.sharding import Mesh, PartitionSpec as P

HEAD_SIZE = 128
CLUSTER = 256


def cluster_attend(q, k, v, dq, dk, dv, pos):
    scaling_multiplier = HEAD_SIZE ** (-0.5)
    logit_scores = (
        jnp.einsum("qe,ke->qk", q, k, preferred_element_type=jnp.float32) * scaling_multiplier
    )
    score_tangent_values = (
        jnp.einsum("qe,ke->qk", dq, k, preferred_element_type=jnp.float32)
        + jnp.einsum("qe,ke->qk", q, dk, preferred_element_type=jnp.float32)
    ) * scaling_multiplier
    visible = pos[None, :] <= pos[:, None]
    masked = jnp.where(visible, logit_scores, -jnp.inf)
    top_score = jnp.max(masked, axis=-1, keepdims=True)
    expo = jnp.where(visible, jnp.exp(masked - top_score), 0.0)
    attn_probs = expo / jnp.sum(expo, axis=-1, keepdims=True)
    probs_half = attn_probs.astype(jnp.bfloat16)
    attended_values = jnp.einsum(
        "qk,ke->qe", probs_half, v, preferred_element_type=jnp.float32
    ).astype(jnp.bfloat16)
    tangent_probs = attn_probs * (
        score_tangent_values - jnp.sum(attn_probs * score_tangent_values, axis=-1, keepdims=True)
    )
    tangent_half = tangent_probs.astype(jnp.bfloat16)
    attended_tangent_sum = (
        jnp.einsum("qk,ke->qe", tangent_half, v, preferred_element_type=jnp.float32)
        + jnp.einsum("qk,ke->qe", probs_half, dv, preferred_element_type=jnp.float32)
    ).astype(jnp.bfloat16)
    return attended_values, attended_tangent_sum


def body(query_rows, key_rows, value_rows, query_tan, key_tan, value_tan, routes, out_weight):
    tok_dev = routes.shape[0]
    heads_here = routes.shape[1]
    n_seq = lax.axis_size("seq")
    inputs = (query_rows, key_rows, value_rows, query_tan, key_tan, value_tan)
    n_in = len(inputs)

    zh = lax.axis_index("zh")
    n_g = lax.axis_size("yc")
    blk = out_weight.shape[0]
    j_idx = lax.axis_index("yc")

    def cols_for(j):
        return jnp.concatenate(
            [
                lax.dynamic_slice_in_dim(out_weight, j * blk, blk, axis=1),
                lax.dynamic_slice_in_dim(out_weight, (n_g + j) * blk, blk, axis=1),
            ],
            axis=1,
        )

    n_y = n_g // 2
    def pair_cols(j):
        return jnp.concatenate([cols_for(j), cols_for(jnp.bitwise_xor(j, 1))], axis=1)

    w_pairs = [pair_cols(j_idx)]
    for m in range(1, n_y):
        w_pairs.append(
            lax.ppermute(
                pair_cols((j_idx + 2 * m) % n_g),
                "yc",
                perm=[(i, (i + 2 * m) % n_g) for i in range(n_g)],
            )
        )
    w_same = [p[:, :2 * blk] for p in w_pairs]
    w_other = lax.ppermute(
        jnp.stack([p[:, 2 * blk:] for p in w_pairs]), "yc", perm=[(i, i ^ 1) for i in range(n_g)]
    )
    w_blocks = (jnp.stack(w_same), w_other)

    token = lax.broadcasted_iota(jnp.int32, routes.shape, 0)
    key = (routes // CLUSTER) * tok_dev + token
    rank = jnp.sum((key[None, :, :] < key[:, None, :]).astype(jnp.int32), axis=1)
    slots = lax.broadcasted_iota(jnp.int32, (tok_dev, tok_dev), 0)
    perm = jnp.stack(
        [(rank[None, :, h] == slots).astype(jnp.bfloat16) for h in range(heads_here)]
    )

    per_head = jnp.stack(
        [
            jnp.concatenate([m[:, h * HEAD_SIZE:(h + 1) * HEAD_SIZE] for m in inputs], axis=1)
            for h in range(heads_here)
        ]
    )
    width = per_head.shape[2]
    sorted_rows = jnp.concatenate(
        [
            jnp.dot(perm[h], per_head[h], preferred_element_type=jnp.float32).astype(jnp.bfloat16)
            for h in range(heads_here)
        ],
        axis=1,
    )
    arrived = lax.all_to_all(sorted_rows, "seq", split_axis=0, concat_axis=0, tiled=True)

    pos = lax.broadcasted_iota(jnp.int32, (tok_dev,), 0)
    outs = []
    for h in range(heads_here):
        base = h * width
        cols = [arrived[:, base + i * HEAD_SIZE:base + (i + 1) * HEAD_SIZE] for i in range(n_in)]
        a, at = cluster_attend(*cols, pos)
        outs.append(jnp.concatenate([a, at], axis=1))
    back = jnp.concatenate(outs, axis=1)
    returned = lax.all_to_all(back, "seq", split_axis=0, concat_axis=0, tiled=True)

    restored = [
        jnp.dot(
            perm[h].T,
            returned[:, h * 2 * HEAD_SIZE:(h + 1) * 2 * HEAD_SIZE],
            preferred_element_type=jnp.float32,
        ).astype(jnp.bfloat16)
        for h in range(heads_here)
    ]
    local = jnp.stack(
        [
            jnp.concatenate([r[:, o * HEAD_SIZE:(o + 1) * HEAD_SIZE] for r in restored], axis=1)
            for o in range(2)
        ]
    )

    flat = jnp.concatenate([local[0], local[1]], axis=1)
    same = jnp.stack(
        [flat]
        + [
            lax.ppermute(flat, "yc", perm=[(i, (i + 2 * m) % n_g) for i in range(n_g)])
            for m in range(1, n_y)
        ]
    )
    other = lax.ppermute(same, "yc", perm=[(i, i ^ 1) for i in range(n_g)])
    shape4 = (n_y, tok_dev, 2, heads_here * HEAD_SIZE)
    projected = jnp.einsum(
        "kcd,kioc->odi", w_blocks[0], same.reshape(shape4), preferred_element_type=jnp.float32
    ) + jnp.einsum(
        "kcd,kioc->odi", w_blocks[1], other.reshape(shape4), preferred_element_type=jnp.float32
    )
    mine = lax.dynamic_slice_in_dim(projected, zh * blk, blk, axis=1)
    theirs = lax.dynamic_slice_in_dim(projected, (1 - zh) * blk, blk, axis=1)
    other_half = lax.ppermute(theirs.astype(jnp.bfloat16), "zh", perm=[(0, 1), (1, 0)])
    summed = mine + other_half.astype(jnp.float32)
    return tuple(summed[o].T.astype(jnp.bfloat16) for o in range(2))


def solution(mesh):
    n_seq, n_ten = mesh.devices.shape
    split = Mesh(mesh.devices.reshape(n_seq, 2, n_ten // 2), ("seq", "zh", "yc"))
    rows = P("seq", ("zh", "yc"))
    return jax.shard_map(
        body,
        mesh=split,
        in_specs=(rows, rows, rows, rows, rows, rows, rows, P(("zh", "yc"), None)),
        out_specs=(rows, rows),
        check_vma=False,
    )
```

```python
import jax
import jax.numpy as jnp
from jax import lax
from jax.experimental import pallas as pl
from jax.sharding import Mesh, PartitionSpec as P

HEAD_SIZE = 128
CLUSTER = 256


def cluster_attend(q, k, v, dq, dk, dv, pos):
    scaling_multiplier = HEAD_SIZE ** (-0.5)
    logit_scores = (
        jnp.einsum("qe,ke->qk", q, k, preferred_element_type=jnp.float32) * scaling_multiplier
    )
    score_tangent_values = (
        jnp.einsum("qe,ke->qk", dq, k, preferred_element_type=jnp.float32)
        + jnp.einsum("qe,ke->qk", q, dk, preferred_element_type=jnp.float32)
    ) * scaling_multiplier
    visible = pos[None, :] <= pos[:, None]
    masked = jnp.where(visible, logit_scores, -jnp.inf)
    top_score = jnp.max(masked, axis=-1, keepdims=True)
    expo = jnp.where(visible, jnp.exp(masked - top_score), 0.0)
    attn_probs = expo / jnp.sum(expo, axis=-1, keepdims=True)
    probs_half = attn_probs.astype(jnp.bfloat16)
    attended_values = jnp.einsum(
        "qk,ke->qe", probs_half, v, preferred_element_type=jnp.float32
    ).astype(jnp.bfloat16)
    tangent_probs = attn_probs * (
        score_tangent_values - jnp.sum(attn_probs * score_tangent_values, axis=-1, keepdims=True)
    )
    tangent_half = tangent_probs.astype(jnp.bfloat16)
    attended_tangent_sum = (
        jnp.einsum("qk,ke->qe", tangent_half, v, preferred_element_type=jnp.float32)
        + jnp.einsum("qk,ke->qe", probs_half, dv, preferred_element_type=jnp.float32)
    ).astype(jnp.bfloat16)
    return attended_values, attended_tangent_sum


def send_rows_kernel(key_col_ref, key_row_ref, *refs):
    *ins, rows_ref, perm_ref = refs
    tok = key_col_ref.shape[0]
    heads = key_col_ref.shape[1]
    slots = lax.broadcasted_iota(jnp.int32, (tok, tok), 0)
    for h in range(heads):
        less = key_col_ref[:, h:h + 1] < key_row_ref[h:h + 1, :]
        rank = jnp.sum(less.astype(jnp.int32), axis=0, keepdims=True)
        perm = (slots == rank).astype(jnp.bfloat16)
        perm_ref[h] = perm
        for m, x_ref in enumerate(ins):
            col = (h * len(ins) + m) * HEAD_SIZE
            rows_ref[:, col:col + HEAD_SIZE] = jnp.dot(
                perm, x_ref[:, h * HEAD_SIZE:(h + 1) * HEAD_SIZE],
                preferred_element_type=jnp.float32,
            ).astype(jnp.bfloat16)


def body(query_rows, key_rows, value_rows, query_tan, key_tan, value_tan, routes, out_weight):
    tok_dev = routes.shape[0]
    heads_here = routes.shape[1]
    n_seq = lax.axis_size("seq")
    inputs = (query_rows, key_rows, value_rows, query_tan, key_tan, value_tan)
    n_in = len(inputs)

    zh = lax.axis_index("zh")
    n_g = lax.axis_size("yc")
    blk = out_weight.shape[0]
    j_idx = lax.axis_index("yc")

    def cols_for(j):
        return jnp.concatenate(
            [
                lax.dynamic_slice_in_dim(out_weight, j * blk, blk, axis=1),
                lax.dynamic_slice_in_dim(out_weight, (n_g + j) * blk, blk, axis=1),
            ],
            axis=1,
        )

    n_y = n_g // 2
    def pair_cols(j):
        return jnp.concatenate([cols_for(j), cols_for(jnp.bitwise_xor(j, 1))], axis=1)

    w_pairs = [pair_cols(j_idx)]
    for m in range(1, n_y):
        w_pairs.append(
            lax.ppermute(
                pair_cols((j_idx + 2 * m) % n_g),
                "yc",
                perm=[(i, (i + 2 * m) % n_g) for i in range(n_g)],
            )
        )
    w_same = [p[:, :2 * blk] for p in w_pairs]
    w_other = lax.ppermute(
        jnp.stack([p[:, 2 * blk:] for p in w_pairs]), "yc", perm=[(i, i ^ 1) for i in range(n_g)]
    )
    w_blocks = (jnp.stack(w_same), w_other)

    token = lax.broadcasted_iota(jnp.int32, routes.shape, 0)
    key = (routes // CLUSTER) * tok_dev + token
    width = n_in * HEAD_SIZE
    sorted_rows, perm = pl.pallas_call(
        send_rows_kernel,
        out_shape=(
            jax.ShapeDtypeStruct((tok_dev, heads_here * width), jnp.bfloat16),
            jax.ShapeDtypeStruct((heads_here, tok_dev, tok_dev), jnp.bfloat16),
        ),
    )(key, key.T, *inputs)
    arrived = lax.all_to_all(sorted_rows, "seq", split_axis=0, concat_axis=0, tiled=True)

    pos = lax.broadcasted_iota(jnp.int32, (tok_dev,), 0)
    outs = []
    for h in range(heads_here):
        base = h * width
        cols = [arrived[:, base + i * HEAD_SIZE:base + (i + 1) * HEAD_SIZE] for i in range(n_in)]
        a, at = cluster_attend(*cols, pos)
        outs.append(jnp.concatenate([a, at], axis=1))
    back = jnp.concatenate(outs, axis=1)
    returned = lax.all_to_all(back, "seq", split_axis=0, concat_axis=0, tiled=True)

    restored = [
        jnp.dot(
            perm[h].T,
            returned[:, h * 2 * HEAD_SIZE:(h + 1) * 2 * HEAD_SIZE],
            preferred_element_type=jnp.float32,
        ).astype(jnp.bfloat16)
        for h in range(heads_here)
    ]
    local = jnp.stack(
        [
            jnp.concatenate([r[:, o * HEAD_SIZE:(o + 1) * HEAD_SIZE] for r in restored], axis=1)
            for o in range(2)
        ]
    )

    flat = jnp.concatenate([local[0], local[1]], axis=1)
    same = jnp.stack(
        [flat]
        + [
            lax.ppermute(flat, "yc", perm=[(i, (i + 2 * m) % n_g) for i in range(n_g)])
            for m in range(1, n_y)
        ]
    )
    other = lax.ppermute(same, "yc", perm=[(i, i ^ 1) for i in range(n_g)])
    shape4 = (n_y, tok_dev, 2, heads_here * HEAD_SIZE)
    projected = jnp.einsum(
        "kcd,kioc->odi", w_blocks[0], same.reshape(shape4), preferred_element_type=jnp.float32
    ) + jnp.einsum(
        "kcd,kioc->odi", w_blocks[1], other.reshape(shape4), preferred_element_type=jnp.float32
    )
    mine = lax.dynamic_slice_in_dim(projected, zh * blk, blk, axis=1)
    theirs = lax.dynamic_slice_in_dim(projected, (1 - zh) * blk, blk, axis=1)
    other_half = lax.ppermute(theirs.astype(jnp.bfloat16), "zh", perm=[(0, 1), (1, 0)])
    summed = mine + other_half.astype(jnp.float32)
    return tuple(summed[o].T.astype(jnp.bfloat16) for o in range(2))


def solution(mesh):
    n_seq, n_ten = mesh.devices.shape
    split = Mesh(mesh.devices.reshape(n_seq, 2, n_ten // 2), ("seq", "zh", "yc"))
    rows = P("seq", ("zh", "yc"))
    return jax.shard_map(
        body,
        mesh=split,
        in_specs=(rows, rows, rows, rows, rows, rows, rows, P(("zh", "yc"), None)),
        out_specs=(rows, rows),
        check_vma=False,
    )
```

```python
import jax
import jax.numpy as jnp
from jax import lax
from jax.experimental import pallas as pl
from jax.sharding import Mesh, PartitionSpec as P

HEAD_SIZE = 128
CLUSTER = 256


def cluster_attend(q, k, v, dq, dk, dv, pos):
    scaling_multiplier = HEAD_SIZE ** (-0.5)
    logit_scores = (
        jnp.einsum("qe,ke->qk", q, k, preferred_element_type=jnp.float32) * scaling_multiplier
    )
    score_tangent_values = (
        jnp.einsum("qe,ke->qk", dq, k, preferred_element_type=jnp.float32)
        + jnp.einsum("qe,ke->qk", q, dk, preferred_element_type=jnp.float32)
    ) * scaling_multiplier
    visible = pos[None, :] <= pos[:, None]
    masked = jnp.where(visible, logit_scores, -jnp.inf)
    top_score = jnp.max(masked, axis=-1, keepdims=True)
    expo = jnp.where(visible, jnp.exp(masked - top_score), 0.0)
    attn_probs = expo / jnp.sum(expo, axis=-1, keepdims=True)
    probs_half = attn_probs.astype(jnp.bfloat16)
    attended_values = jnp.einsum(
        "qk,ke->qe", probs_half, v, preferred_element_type=jnp.float32
    ).astype(jnp.bfloat16)
    tangent_probs = attn_probs * (
        score_tangent_values - jnp.sum(attn_probs * score_tangent_values, axis=-1, keepdims=True)
    )
    tangent_half = tangent_probs.astype(jnp.bfloat16)
    attended_tangent_sum = (
        jnp.einsum("qk,ke->qe", tangent_half, v, preferred_element_type=jnp.float32)
        + jnp.einsum("qk,ke->qe", probs_half, dv, preferred_element_type=jnp.float32)
    ).astype(jnp.bfloat16)
    return attended_values, attended_tangent_sum


def send_rows_kernel(routes_ref, *refs):
    *ins, rows_ref, perm_ref = refs
    tok = routes_ref.shape[0]
    heads = routes_ref.shape[1]
    slots = lax.broadcasted_iota(jnp.int32, (tok, tok), 0)
    lanes = lax.broadcasted_iota(jnp.int32, (tok, tok), 1)
    for h in range(heads):
        cluster_col = routes_ref[:, h:h + 1] // CLUSTER
        cluster_row = jnp.sum(
            jnp.where(slots == lanes, cluster_col, 0), axis=0, keepdims=True
        )
        key_col = cluster_col * tok + slots[:, :1]
        key_row = cluster_row * tok + lanes[:1, :]
        less = key_col < key_row
        rank = jnp.sum(less.astype(jnp.int32), axis=0, keepdims=True)
        perm = (slots == rank).astype(jnp.bfloat16)
        perm_ref[h] = perm
        for m, x_ref in enumerate(ins):
            col = (h * len(ins) + m) * HEAD_SIZE
            rows_ref[:, col:col + HEAD_SIZE] = jnp.dot(
                perm, x_ref[:, h * HEAD_SIZE:(h + 1) * HEAD_SIZE],
                preferred_element_type=jnp.float32,
            ).astype(jnp.bfloat16)

def body(query_rows, key_rows, value_rows, query_tan, key_tan, value_tan, routes, out_weight):
    tok_dev = routes.shape[0]
    heads_here = routes.shape[1]
    n_seq = lax.axis_size("seq")
    inputs = (query_rows, key_rows, value_rows, query_tan, key_tan, value_tan)
    n_in = len(inputs)

    zh = lax.axis_index("zh")
    n_g = lax.axis_size("yc")
    blk = out_weight.shape[0]
    j_idx = lax.axis_index("yc")

    def cols_for(j):
        return jnp.concatenate(
            [
                lax.dynamic_slice_in_dim(out_weight, j * blk, blk, axis=1),
                lax.dynamic_slice_in_dim(out_weight, (n_g + j) * blk, blk, axis=1),
            ],
            axis=1,
        )

    n_y = n_g // 2
    def pair_cols(j):
        return jnp.concatenate([cols_for(j), cols_for(jnp.bitwise_xor(j, 1))], axis=1)

    w_pairs = [pair_cols(j_idx)]
    for m in range(1, n_y):
        w_pairs.append(
            lax.ppermute(
                pair_cols((j_idx + 2 * m) % n_g),
                "yc",
                perm=[(i, (i + 2 * m) % n_g) for i in range(n_g)],
            )
        )
    w_same = [p[:, :2 * blk] for p in w_pairs]
    w_other = lax.ppermute(
        jnp.stack([p[:, 2 * blk:] for p in w_pairs]), "yc", perm=[(i, i ^ 1) for i in range(n_g)]
    )
    w_blocks = (jnp.stack(w_same), w_other)

    width = n_in * HEAD_SIZE
    sorted_rows, perm = pl.pallas_call(
        send_rows_kernel,
        out_shape=(
            jax.ShapeDtypeStruct((tok_dev, heads_here * width), jnp.bfloat16),
            jax.ShapeDtypeStruct((heads_here, tok_dev, tok_dev), jnp.bfloat16),
        ),
    )(routes, *inputs)
    arrived = lax.all_to_all(sorted_rows, "seq", split_axis=0, concat_axis=0, tiled=True)

    pos = lax.broadcasted_iota(jnp.int32, (tok_dev,), 0)
    outs = []
    for h in range(heads_here):
        base = h * width
        cols = [arrived[:, base + i * HEAD_SIZE:base + (i + 1) * HEAD_SIZE] for i in range(n_in)]
        a, at = cluster_attend(*cols, pos)
        outs.append(jnp.concatenate([a, at], axis=1))
    back = jnp.concatenate(outs, axis=1)
    returned = lax.all_to_all(back, "seq", split_axis=0, concat_axis=0, tiled=True)

    restored = [
        jnp.dot(
            perm[h].T,
            returned[:, h * 2 * HEAD_SIZE:(h + 1) * 2 * HEAD_SIZE],
            preferred_element_type=jnp.float32,
        ).astype(jnp.bfloat16)
        for h in range(heads_here)
    ]
    local = jnp.stack(
        [
            jnp.concatenate([r[:, o * HEAD_SIZE:(o + 1) * HEAD_SIZE] for r in restored], axis=1)
            for o in range(2)
        ]
    )

    flat = jnp.concatenate([local[0], local[1]], axis=1)
    same = jnp.stack(
        [flat]
        + [
            lax.ppermute(flat, "yc", perm=[(i, (i + 2 * m) % n_g) for i in range(n_g)])
            for m in range(1, n_y)
        ]
    )
    other = lax.ppermute(same, "yc", perm=[(i, i ^ 1) for i in range(n_g)])
    shape4 = (n_y, tok_dev, 2, heads_here * HEAD_SIZE)
    projected = jnp.einsum(
        "kcd,kioc->odi", w_blocks[0], same.reshape(shape4), preferred_element_type=jnp.float32
    ) + jnp.einsum(
        "kcd,kioc->odi", w_blocks[1], other.reshape(shape4), preferred_element_type=jnp.float32
    )
    mine = lax.dynamic_slice_in_dim(projected, zh * blk, blk, axis=1)
    theirs = lax.dynamic_slice_in_dim(projected, (1 - zh) * blk, blk, axis=1)
    other_half = lax.ppermute(theirs.astype(jnp.bfloat16), "zh", perm=[(0, 1), (1, 0)])
    summed = mine + other_half.astype(jnp.float32)
    return tuple(summed[o].T.astype(jnp.bfloat16) for o in range(2))


def solution(mesh):
    n_seq, n_ten = mesh.devices.shape
    split = Mesh(mesh.devices.reshape(n_seq, 2, n_ten // 2), ("seq", "zh", "yc"))
    rows = P("seq", ("zh", "yc"))
    return jax.shard_map(
        body,
        mesh=split,
        in_specs=(rows, rows, rows, rows, rows, rows, rows, P(("zh", "yc"), None)),
        out_specs=(rows, rows),
        check_vma=False,
    )
```

```python
import jax
import jax.numpy as jnp
from jax import lax
from jax.experimental import pallas as pl
from jax.sharding import Mesh, PartitionSpec as P

HEAD_SIZE = 128
CLUSTER = 256


def cluster_attend(q, k, v, dq, dk, dv, pos):
    scaling_multiplier = HEAD_SIZE ** (-0.5)
    logit_scores = (
        jnp.einsum("qe,ke->qk", q, k, preferred_element_type=jnp.float32) * scaling_multiplier
    )
    score_tangent_values = (
        jnp.einsum("qe,ke->qk", dq, k, preferred_element_type=jnp.float32)
        + jnp.einsum("qe,ke->qk", q, dk, preferred_element_type=jnp.float32)
    ) * scaling_multiplier
    visible = pos[None, :] <= pos[:, None]
    masked = jnp.where(visible, logit_scores, -jnp.inf)
    top_score = jnp.max(masked, axis=-1, keepdims=True)
    expo = jnp.where(visible, jnp.exp(masked - top_score), 0.0)
    attn_probs = expo / jnp.sum(expo, axis=-1, keepdims=True)
    probs_half = attn_probs.astype(jnp.bfloat16)
    attended_values = jnp.einsum(
        "qk,ke->qe", probs_half, v, preferred_element_type=jnp.float32
    ).astype(jnp.bfloat16)
    tangent_probs = attn_probs * (
        score_tangent_values - jnp.sum(attn_probs * score_tangent_values, axis=-1, keepdims=True)
    )
    tangent_half = tangent_probs.astype(jnp.bfloat16)
    attended_tangent_sum = (
        jnp.einsum("qk,ke->qe", tangent_half, v, preferred_element_type=jnp.float32)
        + jnp.einsum("qk,ke->qe", probs_half, dv, preferred_element_type=jnp.float32)
    ).astype(jnp.bfloat16)
    return attended_values, attended_tangent_sum


def send_rows_kernel(routes_t_ref, *refs):
    *ins, rows_ref, perm_ref = refs
    heads = routes_t_ref.shape[0]
    tok = routes_t_ref.shape[1]
    slots = lax.broadcasted_iota(jnp.int32, (tok, tok), 0)
    lanes = lax.broadcasted_iota(jnp.int32, (tok, tok), 1)
    for h in range(heads):
        cluster_row = routes_t_ref[h:h + 1, :] // CLUSTER
        cluster_col = jnp.sum(
            jnp.where(slots == lanes, cluster_row, 0), axis=1, keepdims=True
        )
        key_col = cluster_col * tok + slots[:, :1]
        key_row = cluster_row * tok + lanes[:1, :]
        less = key_col < key_row
        rank = jnp.sum(less.astype(jnp.int32), axis=0, keepdims=True)
        perm = (slots == rank).astype(jnp.bfloat16)
        perm_ref[h] = perm
        for m, x_ref in enumerate(ins):
            col = (h * len(ins) + m) * HEAD_SIZE
            rows_ref[:, col:col + HEAD_SIZE] = jnp.dot(
                perm, x_ref[:, h * HEAD_SIZE:(h + 1) * HEAD_SIZE],
                preferred_element_type=jnp.float32,
            ).astype(jnp.bfloat16)

def body(query_rows, key_rows, value_rows, query_tan, key_tan, value_tan, routes, out_weight):
    tok_dev = routes.shape[0]
    heads_here = routes.shape[1]
    n_seq = lax.axis_size("seq")
    inputs = (query_rows, key_rows, value_rows, query_tan, key_tan, value_tan)
    n_in = len(inputs)

    zh = lax.axis_index("zh")
    n_g = lax.axis_size("yc")
    blk = out_weight.shape[0]
    j_idx = lax.axis_index("yc")

    def cols_for(j):
        return jnp.concatenate(
            [
                lax.dynamic_slice_in_dim(out_weight, j * blk, blk, axis=1),
                lax.dynamic_slice_in_dim(out_weight, (n_g + j) * blk, blk, axis=1),
            ],
            axis=1,
        )

    n_y = n_g // 2
    def pair_cols(j):
        return jnp.concatenate([cols_for(j), cols_for(jnp.bitwise_xor(j, 1))], axis=1)

    w_pairs = [pair_cols(j_idx)]
    for m in range(1, n_y):
        w_pairs.append(
            lax.ppermute(
                pair_cols((j_idx + 2 * m) % n_g),
                "yc",
                perm=[(i, (i + 2 * m) % n_g) for i in range(n_g)],
            )
        )
    w_same = [p[:, :2 * blk] for p in w_pairs]
    w_other = lax.ppermute(
        jnp.stack([p[:, 2 * blk:] for p in w_pairs]), "yc", perm=[(i, i ^ 1) for i in range(n_g)]
    )
    w_blocks = (jnp.stack(w_same), w_other)

    width = n_in * HEAD_SIZE
    sorted_rows, perm = pl.pallas_call(
        send_rows_kernel,
        out_shape=(
            jax.ShapeDtypeStruct((tok_dev, heads_here * width), jnp.bfloat16),
            jax.ShapeDtypeStruct((heads_here, tok_dev, tok_dev), jnp.bfloat16),
        ),
    )(routes.T, *inputs)
    arrived = lax.all_to_all(sorted_rows, "seq", split_axis=0, concat_axis=0, tiled=True)

    pos = lax.broadcasted_iota(jnp.int32, (tok_dev,), 0)
    outs = []
    for h in range(heads_here):
        base = h * width
        cols = [arrived[:, base + i * HEAD_SIZE:base + (i + 1) * HEAD_SIZE] for i in range(n_in)]
        a, at = cluster_attend(*cols, pos)
        outs.append(jnp.concatenate([a, at], axis=1))
    back = jnp.concatenate(outs, axis=1)
    returned = lax.all_to_all(back, "seq", split_axis=0, concat_axis=0, tiled=True)

    restored = [
        jnp.dot(
            perm[h].T,
            returned[:, h * 2 * HEAD_SIZE:(h + 1) * 2 * HEAD_SIZE],
            preferred_element_type=jnp.float32,
        ).astype(jnp.bfloat16)
        for h in range(heads_here)
    ]
    local = jnp.stack(
        [
            jnp.concatenate([r[:, o * HEAD_SIZE:(o + 1) * HEAD_SIZE] for r in restored], axis=1)
            for o in range(2)
        ]
    )

    flat = jnp.concatenate([local[0], local[1]], axis=1)
    same = jnp.stack(
        [flat]
        + [
            lax.ppermute(flat, "yc", perm=[(i, (i + 2 * m) % n_g) for i in range(n_g)])
            for m in range(1, n_y)
        ]
    )
    other = lax.ppermute(same, "yc", perm=[(i, i ^ 1) for i in range(n_g)])
    shape4 = (n_y, tok_dev, 2, heads_here * HEAD_SIZE)
    projected = jnp.einsum(
        "kcd,kioc->odi", w_blocks[0], same.reshape(shape4), preferred_element_type=jnp.float32
    ) + jnp.einsum(
        "kcd,kioc->odi", w_blocks[1], other.reshape(shape4), preferred_element_type=jnp.float32
    )
    mine = lax.dynamic_slice_in_dim(projected, zh * blk, blk, axis=1)
    theirs = lax.dynamic_slice_in_dim(projected, (1 - zh) * blk, blk, axis=1)
    other_half = lax.ppermute(theirs.astype(jnp.bfloat16), "zh", perm=[(0, 1), (1, 0)])
    summed = mine + other_half.astype(jnp.float32)
    return tuple(summed[o].T.astype(jnp.bfloat16) for o in range(2))


def solution(mesh):
    n_seq, n_ten = mesh.devices.shape
    split = Mesh(mesh.devices.reshape(n_seq, 2, n_ten // 2), ("seq", "zh", "yc"))
    rows = P("seq", ("zh", "yc"))
    return jax.shard_map(
        body,
        mesh=split,
        in_specs=(rows, rows, rows, rows, rows, rows, rows, P(("zh", "yc"), None)),
        out_specs=(rows, rows),
        check_vma=False,
    )
```

```python
import jax
import jax.numpy as jnp
from jax import lax
from jax.experimental import pallas as pl
from jax.sharding import Mesh, PartitionSpec as P

HEAD_SIZE = 128
CLUSTER = 256


def cluster_attend(q, k, v, dq, dk, dv, pos):
    scaling_multiplier = HEAD_SIZE ** (-0.5)
    logit_scores = (
        jnp.einsum("qe,ke->qk", q, k, preferred_element_type=jnp.float32) * scaling_multiplier
    )
    score_tangent_values = (
        jnp.einsum("qe,ke->qk", dq, k, preferred_element_type=jnp.float32)
        + jnp.einsum("qe,ke->qk", q, dk, preferred_element_type=jnp.float32)
    ) * scaling_multiplier
    visible = pos[None, :] <= pos[:, None]
    masked = jnp.where(visible, logit_scores, -jnp.inf)
    top_score = jnp.max(masked, axis=-1, keepdims=True)
    expo = jnp.where(visible, jnp.exp(masked - top_score), 0.0)
    attn_probs = expo / jnp.sum(expo, axis=-1, keepdims=True)
    probs_half = attn_probs.astype(jnp.bfloat16)
    attended_values = jnp.einsum(
        "qk,ke->qe", probs_half, v, preferred_element_type=jnp.float32
    ).astype(jnp.bfloat16)
    tangent_probs = attn_probs * (
        score_tangent_values - jnp.sum(attn_probs * score_tangent_values, axis=-1, keepdims=True)
    )
    tangent_half = tangent_probs.astype(jnp.bfloat16)
    attended_tangent_sum = (
        jnp.einsum("qk,ke->qe", tangent_half, v, preferred_element_type=jnp.float32)
        + jnp.einsum("qk,ke->qe", probs_half, dv, preferred_element_type=jnp.float32)
    ).astype(jnp.bfloat16)
    return attended_values, attended_tangent_sum


def send_rows_kernel(routes_t_ref, *refs):
    *ins, rows_ref, perm_ref = refs
    heads = routes_t_ref.shape[0]
    tok = routes_t_ref.shape[1]
    slots = lax.broadcasted_iota(jnp.int32, (tok, tok), 0)
    lanes = lax.broadcasted_iota(jnp.int32, (tok, tok), 1)
    for h in range(heads):
        cluster_row = routes_t_ref[h:h + 1, :] // CLUSTER
        cluster_col = jnp.sum(
            jnp.where(slots == lanes, cluster_row, 0), axis=1, keepdims=True
        )
        key_col = cluster_col * tok + slots[:, :1]
        key_row = cluster_row * tok + lanes[:1, :]
        less = key_col < key_row
        rank = jnp.sum(less.astype(jnp.int32), axis=0, keepdims=True)
        perm = (slots == rank).astype(jnp.bfloat16)
        perm_ref[h] = perm
        for m, x_ref in enumerate(ins):
            col = (h * len(ins) + m) * HEAD_SIZE
            rows_ref[:, col:col + HEAD_SIZE] = jnp.dot(
                perm, x_ref[:, h * HEAD_SIZE:(h + 1) * HEAD_SIZE],
                preferred_element_type=jnp.float32,
            ).astype(jnp.bfloat16)

def attend_kernel(arr_ref, out_ref):
    tok = arr_ref.shape[0]
    heads = out_ref.shape[1] // (2 * HEAD_SIZE)
    n_in = arr_ref.shape[1] // (heads * HEAD_SIZE)
    scale = HEAD_SIZE ** (-0.5)
    nt = (((1,), (1,)), ((), ()))
    visible = lax.broadcasted_iota(jnp.int32, (tok, tok), 1) <= lax.broadcasted_iota(
        jnp.int32, (tok, tok), 0
    )
    for h in range(heads):
        q, k, v, dq, dk, dv = [
            arr_ref[:, (h * n_in + i) * HEAD_SIZE:(h * n_in + i + 1) * HEAD_SIZE]
            for i in range(n_in)
        ]
        logits = lax.dot_general(q, k, nt, preferred_element_type=jnp.float32) * scale
        tangent = (
            lax.dot_general(dq, k, nt, preferred_element_type=jnp.float32)
            + lax.dot_general(q, dk, nt, preferred_element_type=jnp.float32)
        ) * scale
        masked = jnp.where(visible, logits, -jnp.inf)
        top = jnp.max(masked, axis=-1, keepdims=True)
        expo = jnp.where(visible, jnp.exp(masked - top), 0.0)
        probs = expo / jnp.sum(expo, axis=-1, keepdims=True)
        probs_half = probs.astype(jnp.bfloat16)
        base = h * 2 * HEAD_SIZE
        out_ref[:, base:base + HEAD_SIZE] = jnp.dot(
            probs_half, v, preferred_element_type=jnp.float32
        ).astype(jnp.bfloat16)
        tangent_probs = probs * (tangent - jnp.sum(probs * tangent, axis=-1, keepdims=True))
        tangent_half = tangent_probs.astype(jnp.bfloat16)
        out_ref[:, base + HEAD_SIZE:base + 2 * HEAD_SIZE] = (
            jnp.dot(tangent_half, v, preferred_element_type=jnp.float32)
            + jnp.dot(probs_half, dv, preferred_element_type=jnp.float32)
        ).astype(jnp.bfloat16)


def body(query_rows, key_rows, value_rows, query_tan, key_tan, value_tan, routes, out_weight):
    tok_dev = routes.shape[0]
    heads_here = routes.shape[1]
    n_seq = lax.axis_size("seq")
    inputs = (query_rows, key_rows, value_rows, query_tan, key_tan, value_tan)
    n_in = len(inputs)

    zh = lax.axis_index("zh")
    n_g = lax.axis_size("yc")
    blk = out_weight.shape[0]
    j_idx = lax.axis_index("yc")

    def cols_for(j):
        return jnp.concatenate(
            [
                lax.dynamic_slice_in_dim(out_weight, j * blk, blk, axis=1),
                lax.dynamic_slice_in_dim(out_weight, (n_g + j) * blk, blk, axis=1),
            ],
            axis=1,
        )

    n_y = n_g // 2
    def pair_cols(j):
        return jnp.concatenate([cols_for(j), cols_for(jnp.bitwise_xor(j, 1))], axis=1)

    w_pairs = [pair_cols(j_idx)]
    for m in range(1, n_y):
        w_pairs.append(
            lax.ppermute(
                pair_cols((j_idx + 2 * m) % n_g),
                "yc",
                perm=[(i, (i + 2 * m) % n_g) for i in range(n_g)],
            )
        )
    w_same = [p[:, :2 * blk] for p in w_pairs]
    w_other = lax.ppermute(
        jnp.stack([p[:, 2 * blk:] for p in w_pairs]), "yc", perm=[(i, i ^ 1) for i in range(n_g)]
    )
    w_blocks = (jnp.stack(w_same), w_other)

    width = n_in * HEAD_SIZE
    sorted_rows, perm = pl.pallas_call(
        send_rows_kernel,
        out_shape=(
            jax.ShapeDtypeStruct((tok_dev, heads_here * width), jnp.bfloat16),
            jax.ShapeDtypeStruct((heads_here, tok_dev, tok_dev), jnp.bfloat16),
        ),
    )(routes.T, *inputs)
    arrived = lax.all_to_all(sorted_rows, "seq", split_axis=0, concat_axis=0, tiled=True)

    back = pl.pallas_call(
        attend_kernel,
        out_shape=jax.ShapeDtypeStruct((tok_dev, heads_here * 2 * HEAD_SIZE), jnp.bfloat16),
    )(arrived)
    returned = lax.all_to_all(back, "seq", split_axis=0, concat_axis=0, tiled=True)

    restored = [
        jnp.dot(
            perm[h].T,
            returned[:, h * 2 * HEAD_SIZE:(h + 1) * 2 * HEAD_SIZE],
            preferred_element_type=jnp.float32,
        ).astype(jnp.bfloat16)
        for h in range(heads_here)
    ]
    local = jnp.stack(
        [
            jnp.concatenate([r[:, o * HEAD_SIZE:(o + 1) * HEAD_SIZE] for r in restored], axis=1)
            for o in range(2)
        ]
    )

    flat = jnp.concatenate([local[0], local[1]], axis=1)
    same = jnp.stack(
        [flat]
        + [
            lax.ppermute(flat, "yc", perm=[(i, (i + 2 * m) % n_g) for i in range(n_g)])
            for m in range(1, n_y)
        ]
    )
    other = lax.ppermute(same, "yc", perm=[(i, i ^ 1) for i in range(n_g)])
    shape4 = (n_y, tok_dev, 2, heads_here * HEAD_SIZE)
    projected = jnp.einsum(
        "kcd,kioc->odi", w_blocks[0], same.reshape(shape4), preferred_element_type=jnp.float32
    ) + jnp.einsum(
        "kcd,kioc->odi", w_blocks[1], other.reshape(shape4), preferred_element_type=jnp.float32
    )
    mine = lax.dynamic_slice_in_dim(projected, zh * blk, blk, axis=1)
    theirs = lax.dynamic_slice_in_dim(projected, (1 - zh) * blk, blk, axis=1)
    other_half = lax.ppermute(theirs.astype(jnp.bfloat16), "zh", perm=[(0, 1), (1, 0)])
    summed = mine + other_half.astype(jnp.float32)
    return tuple(summed[o].T.astype(jnp.bfloat16) for o in range(2))


def solution(mesh):
    n_seq, n_ten = mesh.devices.shape
    split = Mesh(mesh.devices.reshape(n_seq, 2, n_ten // 2), ("seq", "zh", "yc"))
    rows = P("seq", ("zh", "yc"))
    return jax.shard_map(
        body,
        mesh=split,
        in_specs=(rows, rows, rows, rows, rows, rows, rows, P(("zh", "yc"), None)),
        out_specs=(rows, rows),
        check_vma=False,
    )
```

```python
import jax
import jax.numpy as jnp
from jax import lax
from jax.experimental import pallas as pl
from jax.sharding import Mesh, PartitionSpec as P

HEAD_SIZE = 128
CLUSTER = 256


def cluster_attend(q, k, v, dq, dk, dv, pos):
    scaling_multiplier = HEAD_SIZE ** (-0.5)
    logit_scores = (
        jnp.einsum("qe,ke->qk", q, k, preferred_element_type=jnp.float32) * scaling_multiplier
    )
    score_tangent_values = (
        jnp.einsum("qe,ke->qk", dq, k, preferred_element_type=jnp.float32)
        + jnp.einsum("qe,ke->qk", q, dk, preferred_element_type=jnp.float32)
    ) * scaling_multiplier
    visible = pos[None, :] <= pos[:, None]
    masked = jnp.where(visible, logit_scores, -jnp.inf)
    top_score = jnp.max(masked, axis=-1, keepdims=True)
    expo = jnp.where(visible, jnp.exp(masked - top_score), 0.0)
    attn_probs = expo / jnp.sum(expo, axis=-1, keepdims=True)
    probs_half = attn_probs.astype(jnp.bfloat16)
    attended_values = jnp.einsum(
        "qk,ke->qe", probs_half, v, preferred_element_type=jnp.float32
    ).astype(jnp.bfloat16)
    tangent_probs = attn_probs * (
        score_tangent_values - jnp.sum(attn_probs * score_tangent_values, axis=-1, keepdims=True)
    )
    tangent_half = tangent_probs.astype(jnp.bfloat16)
    attended_tangent_sum = (
        jnp.einsum("qk,ke->qe", tangent_half, v, preferred_element_type=jnp.float32)
        + jnp.einsum("qk,ke->qe", probs_half, dv, preferred_element_type=jnp.float32)
    ).astype(jnp.bfloat16)
    return attended_values, attended_tangent_sum


def send_rows_kernel(routes_t_ref, *refs):
    *ins, rows_ref, perm_ref = refs
    heads = routes_t_ref.shape[0]
    tok = routes_t_ref.shape[1]
    slots = lax.broadcasted_iota(jnp.int32, (tok, tok), 0)
    lanes = lax.broadcasted_iota(jnp.int32, (tok, tok), 1)
    for h in range(heads):
        cluster_row = routes_t_ref[h:h + 1, :] // CLUSTER
        cluster_col = jnp.sum(
            jnp.where(slots == lanes, cluster_row, 0), axis=1, keepdims=True
        )
        key_col = cluster_col * tok + slots[:, :1]
        key_row = cluster_row * tok + lanes[:1, :]
        less = key_col < key_row
        rank = jnp.sum(less.astype(jnp.int32), axis=0, keepdims=True)
        perm = (slots == rank).astype(jnp.bfloat16)
        perm_ref[h] = perm
        for m, x_ref in enumerate(ins):
            col = (h * len(ins) + m) * HEAD_SIZE
            rows_ref[:, col:col + HEAD_SIZE] = jnp.dot(
                perm, x_ref[:, h * HEAD_SIZE:(h + 1) * HEAD_SIZE],
                preferred_element_type=jnp.float32,
            ).astype(jnp.bfloat16)

def body(query_rows, key_rows, value_rows, query_tan, key_tan, value_tan, routes, out_weight):
    tok_dev = routes.shape[0]
    heads_here = routes.shape[1]
    n_seq = lax.axis_size("seq")
    inputs = (query_rows, key_rows, value_rows, query_tan, key_tan, value_tan)
    n_in = len(inputs)

    zh = lax.axis_index("zh")
    n_g = lax.axis_size("yc")
    blk = out_weight.shape[0]
    j_idx = lax.axis_index("yc")

    def cols_for(j):
        return jnp.concatenate(
            [
                lax.dynamic_slice_in_dim(out_weight, j * blk, blk, axis=1),
                lax.dynamic_slice_in_dim(out_weight, (n_g + j) * blk, blk, axis=1),
            ],
            axis=1,
        )

    n_y = n_g // 2
    def pair_cols(j):
        return jnp.concatenate([cols_for(j), cols_for(jnp.bitwise_xor(j, 1))], axis=1)

    w_pairs = [pair_cols(j_idx)]
    for m in range(1, n_y):
        w_pairs.append(
            lax.ppermute(
                pair_cols((j_idx + 2 * m) % n_g),
                "yc",
                perm=[(i, (i + 2 * m) % n_g) for i in range(n_g)],
            )
        )
    w_same = [p[:, :2 * blk] for p in w_pairs]
    w_other = lax.ppermute(
        jnp.stack([p[:, 2 * blk:] for p in w_pairs]), "yc", perm=[(i, i ^ 1) for i in range(n_g)]
    )
    w_blocks = (jnp.stack(w_same), w_other)

    width = n_in * HEAD_SIZE
    sorted_rows, perm = pl.pallas_call(
        send_rows_kernel,
        out_shape=(
            jax.ShapeDtypeStruct((tok_dev, heads_here * width), jnp.bfloat16),
            jax.ShapeDtypeStruct((heads_here, tok_dev, tok_dev), jnp.bfloat16),
        ),
    )(routes.T, *inputs)
    arrived = lax.all_to_all(sorted_rows, "seq", split_axis=0, concat_axis=0, tiled=True)

    pos = lax.broadcasted_iota(jnp.int32, (tok_dev,), 0)
    outs = []
    for h in range(heads_here):
        base = h * width
        cols = [arrived[:, base + i * HEAD_SIZE:base + (i + 1) * HEAD_SIZE] for i in range(n_in)]
        a, at = cluster_attend(*cols, pos)
        outs.append(jnp.concatenate([a, at], axis=1))
    back = jnp.concatenate(outs, axis=1)
    returned = lax.all_to_all(back, "seq", split_axis=0, concat_axis=0, tiled=True)

    restored = [
        jnp.dot(
            perm[h].T,
            returned[:, h * 2 * HEAD_SIZE:(h + 1) * 2 * HEAD_SIZE],
            preferred_element_type=jnp.float32,
        ).astype(jnp.bfloat16)
        for h in range(heads_here)
    ]
    local = jnp.stack(
        [
            jnp.concatenate([r[:, o * HEAD_SIZE:(o + 1) * HEAD_SIZE] for r in restored], axis=1)
            for o in range(2)
        ]
    )

    flat = jnp.concatenate([local[0], local[1]], axis=1)
    same = jnp.stack(
        [flat]
        + [
            lax.ppermute(flat, "yc", perm=[(i, (i + 2 * m) % n_g) for i in range(n_g)])
            for m in range(1, n_y)
        ]
    )
    other = lax.ppermute(same, "yc", perm=[(i, i ^ 1) for i in range(n_g)])
    shape4 = (n_y, tok_dev, 2, heads_here * HEAD_SIZE)
    from_same = lax.optimization_barrier(
        jnp.einsum(
            "kcd,kioc->odi", w_blocks[0], same.reshape(shape4), preferred_element_type=jnp.float32
        )
    )
    projected = from_same + jnp.einsum(
        "kcd,kioc->odi", w_blocks[1], other.reshape(shape4), preferred_element_type=jnp.float32
    )
    mine = lax.dynamic_slice_in_dim(projected, zh * blk, blk, axis=1)
    theirs = lax.dynamic_slice_in_dim(projected, (1 - zh) * blk, blk, axis=1)
    other_half = lax.ppermute(theirs.astype(jnp.bfloat16), "zh", perm=[(0, 1), (1, 0)])
    summed = mine + other_half.astype(jnp.float32)
    return tuple(summed[o].T.astype(jnp.bfloat16) for o in range(2))


def solution(mesh):
    n_seq, n_ten = mesh.devices.shape
    split = Mesh(mesh.devices.reshape(n_seq, 2, n_ten // 2), ("seq", "zh", "yc"))
    rows = P("seq", ("zh", "yc"))
    return jax.shard_map(
        body,
        mesh=split,
        in_specs=(rows, rows, rows, rows, rows, rows, rows, P(("zh", "yc"), None)),
        out_specs=(rows, rows),
        check_vma=False,
    )
```

```python
import jax
import jax.numpy as jnp
from jax import lax
from jax.experimental import pallas as pl
from jax.sharding import Mesh, PartitionSpec as P

HEAD_SIZE = 128
CLUSTER = 256


def cluster_attend(q, k, v, dq, dk, dv, pos):
    scaling_multiplier = HEAD_SIZE ** (-0.5)
    logit_scores = (
        jnp.einsum("qe,ke->qk", q, k, preferred_element_type=jnp.float32) * scaling_multiplier
    )
    score_tangent_values = (
        jnp.einsum("qe,ke->qk", dq, k, preferred_element_type=jnp.float32)
        + jnp.einsum("qe,ke->qk", q, dk, preferred_element_type=jnp.float32)
    ) * scaling_multiplier
    visible = pos[None, :] <= pos[:, None]
    masked = jnp.where(visible, logit_scores, -jnp.inf)
    top_score = jnp.max(masked, axis=-1, keepdims=True)
    expo = jnp.where(visible, jnp.exp(masked - top_score), 0.0)
    attn_probs = expo / jnp.sum(expo, axis=-1, keepdims=True)
    probs_half = attn_probs.astype(jnp.bfloat16)
    attended_values = jnp.einsum(
        "qk,ke->qe", probs_half, v, preferred_element_type=jnp.float32
    ).astype(jnp.bfloat16)
    tangent_probs = attn_probs * (
        score_tangent_values - jnp.sum(attn_probs * score_tangent_values, axis=-1, keepdims=True)
    )
    tangent_half = tangent_probs.astype(jnp.bfloat16)
    attended_tangent_sum = (
        jnp.einsum("qk,ke->qe", tangent_half, v, preferred_element_type=jnp.float32)
        + jnp.einsum("qk,ke->qe", probs_half, dv, preferred_element_type=jnp.float32)
    ).astype(jnp.bfloat16)
    return attended_values, attended_tangent_sum


def send_rows_kernel(routes_t_ref, *refs):
    *ins, rows_ref, perm_ref = refs
    heads = routes_t_ref.shape[0]
    tok = routes_t_ref.shape[1]
    slots = lax.broadcasted_iota(jnp.int32, (tok, tok), 0)
    lanes = lax.broadcasted_iota(jnp.int32, (tok, tok), 1)
    for h in range(heads):
        cluster_row = routes_t_ref[h:h + 1, :] // CLUSTER
        cluster_col = jnp.sum(
            jnp.where(slots == lanes, cluster_row, 0), axis=1, keepdims=True
        )
        key_col = cluster_col * tok + slots[:, :1]
        key_row = cluster_row * tok + lanes[:1, :]
        less = key_col < key_row
        rank = jnp.sum(less.astype(jnp.int32), axis=0, keepdims=True)
        perm = (slots == rank).astype(jnp.bfloat16)
        perm_ref[h] = perm
        for m, x_ref in enumerate(ins):
            col = (h * len(ins) + m) * HEAD_SIZE
            rows_ref[:, col:col + HEAD_SIZE] = jnp.dot(
                perm, x_ref[:, h * HEAD_SIZE:(h + 1) * HEAD_SIZE],
                preferred_element_type=jnp.float32,
            ).astype(jnp.bfloat16)

def body(query_rows, key_rows, value_rows, query_tan, key_tan, value_tan, routes, out_weight):
    tok_dev = routes.shape[0]
    heads_here = routes.shape[1]
    n_seq = lax.axis_size("seq")
    inputs = (query_rows, key_rows, value_rows, query_tan, key_tan, value_tan)
    n_in = len(inputs)

    zh = lax.axis_index("zh")
    n_g = lax.axis_size("yc")
    blk = out_weight.shape[0]
    j_idx = lax.axis_index("yc")

    def cols_for(j):
        return jnp.concatenate(
            [
                lax.dynamic_slice_in_dim(out_weight, j * blk, blk, axis=1),
                lax.dynamic_slice_in_dim(out_weight, (n_g + j) * blk, blk, axis=1),
            ],
            axis=1,
        )

    n_y = n_g // 2
    def pair_cols(j):
        return jnp.concatenate([cols_for(j), cols_for(jnp.bitwise_xor(j, 1))], axis=1)

    w_pairs = [pair_cols(j_idx)]
    for m in range(1, n_y):
        w_pairs.append(
            lax.ppermute(
                pair_cols((j_idx + 2 * m) % n_g),
                "yc",
                perm=[(i, (i + 2 * m) % n_g) for i in range(n_g)],
            )
        )
    w_same = [p[:, :2 * blk] for p in w_pairs]
    w_other = lax.ppermute(
        jnp.stack([p[:, 2 * blk:] for p in w_pairs]), "yc", perm=[(i, i ^ 1) for i in range(n_g)]
    )
    w_blocks = (jnp.stack(w_same), w_other)

    width = n_in * HEAD_SIZE
    sorted_rows, perm = pl.pallas_call(
        send_rows_kernel,
        out_shape=(
            jax.ShapeDtypeStruct((tok_dev, heads_here * width), jnp.bfloat16),
            jax.ShapeDtypeStruct((heads_here, tok_dev, tok_dev), jnp.bfloat16),
        ),
    )(routes.T, *inputs)
    arrived = lax.all_to_all(sorted_rows, "seq", split_axis=0, concat_axis=0, tiled=True)

    pos = lax.broadcasted_iota(jnp.int32, (tok_dev,), 0)
    outs = []
    for h in range(heads_here):
        base = h * width
        cols = [arrived[:, base + i * HEAD_SIZE:base + (i + 1) * HEAD_SIZE] for i in range(n_in)]
        a, at = cluster_attend(*cols, pos)
        outs.append(jnp.concatenate([a, at], axis=1))
    back = jnp.concatenate(outs, axis=1)
    returned = lax.all_to_all(back, "seq", split_axis=0, concat_axis=0, tiled=True)

    restored = [
        jnp.dot(
            perm[h].T,
            returned[:, h * 2 * HEAD_SIZE:(h + 1) * 2 * HEAD_SIZE],
            preferred_element_type=jnp.float32,
        ).astype(jnp.bfloat16)
        for h in range(heads_here)
    ]
    local = jnp.stack(
        [
            jnp.concatenate([r[:, o * HEAD_SIZE:(o + 1) * HEAD_SIZE] for r in restored], axis=1)
            for o in range(2)
        ]
    )

    same = jnp.stack(
        [local]
        + [
            lax.ppermute(local, "yc", perm=[(i, (i + 2 * m) % n_g) for i in range(n_g)])
            for m in range(1, n_y)
        ],
        axis=1,
    )
    other = lax.ppermute(same, "yc", perm=[(i, i ^ 1) for i in range(n_g)])
    projected = jnp.einsum(
        "kcd,okic->odi", w_blocks[0], same, preferred_element_type=jnp.float32
    ) + jnp.einsum(
        "kcd,okic->odi", w_blocks[1], other, preferred_element_type=jnp.float32
    )
    mine = lax.dynamic_slice_in_dim(projected, zh * blk, blk, axis=1)
    theirs = lax.dynamic_slice_in_dim(projected, (1 - zh) * blk, blk, axis=1)
    other_half = lax.ppermute(theirs.astype(jnp.bfloat16), "zh", perm=[(0, 1), (1, 0)])
    summed = mine + other_half.astype(jnp.float32)
    return tuple(summed[o].T.astype(jnp.bfloat16) for o in range(2))


def solution(mesh):
    n_seq, n_ten = mesh.devices.shape
    split = Mesh(mesh.devices.reshape(n_seq, 2, n_ten // 2), ("seq", "zh", "yc"))
    rows = P("seq", ("zh", "yc"))
    return jax.shard_map(
        body,
        mesh=split,
        in_specs=(rows, rows, rows, rows, rows, rows, rows, P(("zh", "yc"), None)),
        out_specs=(rows, rows),
        check_vma=False,
    )
```

```python
import jax
import jax.numpy as jnp
from jax import lax
from jax.experimental import pallas as pl
from jax.sharding import Mesh, PartitionSpec as P

HEAD_SIZE = 128
CLUSTER = 256


def cluster_attend(q, k, v, dq, dk, dv, pos):
    scaling_multiplier = HEAD_SIZE ** (-0.5)
    logit_scores = (
        jnp.einsum("qe,ke->qk", q, k, preferred_element_type=jnp.float32) * scaling_multiplier
    )
    score_tangent_values = (
        jnp.einsum("qe,ke->qk", dq, k, preferred_element_type=jnp.float32)
        + jnp.einsum("qe,ke->qk", q, dk, preferred_element_type=jnp.float32)
    ) * scaling_multiplier
    visible = pos[None, :] <= pos[:, None]
    masked = jnp.where(visible, logit_scores, -jnp.inf)
    top_score = jnp.max(masked, axis=-1, keepdims=True)
    expo = jnp.where(visible, jnp.exp(masked - top_score), 0.0)
    attn_probs = expo / jnp.sum(expo, axis=-1, keepdims=True)
    probs_half = attn_probs.astype(jnp.bfloat16)
    attended_values = jnp.einsum(
        "qk,ke->qe", probs_half, v, preferred_element_type=jnp.float32
    ).astype(jnp.bfloat16)
    tangent_probs = attn_probs * (
        score_tangent_values - jnp.sum(attn_probs * score_tangent_values, axis=-1, keepdims=True)
    )
    tangent_half = tangent_probs.astype(jnp.bfloat16)
    attended_tangent_sum = (
        jnp.einsum("qk,ke->qe", tangent_half, v, preferred_element_type=jnp.float32)
        + jnp.einsum("qk,ke->qe", probs_half, dv, preferred_element_type=jnp.float32)
    ).astype(jnp.bfloat16)
    return attended_values, attended_tangent_sum


def send_rows_kernel(routes_t_ref, *refs):
    *ins, rows_ref, perm_ref = refs
    heads = routes_t_ref.shape[0]
    tok = routes_t_ref.shape[1]
    slots = lax.broadcasted_iota(jnp.int32, (tok, tok), 0)
    lanes = lax.broadcasted_iota(jnp.int32, (tok, tok), 1)
    for h in range(heads):
        cluster_row = routes_t_ref[h:h + 1, :] // CLUSTER
        cluster_col = jnp.sum(
            jnp.where(slots == lanes, cluster_row, 0), axis=1, keepdims=True
        )
        key_col = cluster_col * tok + slots[:, :1]
        key_row = cluster_row * tok + lanes[:1, :]
        less = key_col < key_row
        rank = jnp.sum(less.astype(jnp.int32), axis=0, keepdims=True)
        perm = (slots == rank).astype(jnp.bfloat16)
        rank_col = jnp.sum((key_row < key_col).astype(jnp.int32), axis=1, keepdims=True)
        perm_ref[h] = (lanes == rank_col).astype(jnp.bfloat16)
        for m, x_ref in enumerate(ins):
            col = (h * len(ins) + m) * HEAD_SIZE
            rows_ref[:, col:col + HEAD_SIZE] = jnp.dot(
                perm, x_ref[:, h * HEAD_SIZE:(h + 1) * HEAD_SIZE],
                preferred_element_type=jnp.float32,
            ).astype(jnp.bfloat16)

def restore_kernel(perm_t_ref, returned_ref, local_ref):
    heads = perm_t_ref.shape[0]
    for h in range(heads):
        for o in range(2):
            src = (h * 2 + o) * HEAD_SIZE
            local_ref[o, :, h * HEAD_SIZE:(h + 1) * HEAD_SIZE] = jnp.dot(
                perm_t_ref[h], returned_ref[:, src:src + HEAD_SIZE],
                preferred_element_type=jnp.float32,
            ).astype(jnp.bfloat16)


def body(query_rows, key_rows, value_rows, query_tan, key_tan, value_tan, routes, out_weight):
    tok_dev = routes.shape[0]
    heads_here = routes.shape[1]
    n_seq = lax.axis_size("seq")
    inputs = (query_rows, key_rows, value_rows, query_tan, key_tan, value_tan)
    n_in = len(inputs)

    zh = lax.axis_index("zh")
    n_g = lax.axis_size("yc")
    blk = out_weight.shape[0]
    j_idx = lax.axis_index("yc")

    def cols_for(j):
        return jnp.concatenate(
            [
                lax.dynamic_slice_in_dim(out_weight, j * blk, blk, axis=1),
                lax.dynamic_slice_in_dim(out_weight, (n_g + j) * blk, blk, axis=1),
            ],
            axis=1,
        )

    n_y = n_g // 2
    def pair_cols(j):
        return jnp.concatenate([cols_for(j), cols_for(jnp.bitwise_xor(j, 1))], axis=1)

    w_pairs = [pair_cols(j_idx)]
    for m in range(1, n_y):
        w_pairs.append(
            lax.ppermute(
                pair_cols((j_idx + 2 * m) % n_g),
                "yc",
                perm=[(i, (i + 2 * m) % n_g) for i in range(n_g)],
            )
        )
    w_same = [p[:, :2 * blk] for p in w_pairs]
    w_other = lax.ppermute(
        jnp.stack([p[:, 2 * blk:] for p in w_pairs]), "yc", perm=[(i, i ^ 1) for i in range(n_g)]
    )
    w_blocks = (jnp.stack(w_same), w_other)

    width = n_in * HEAD_SIZE
    sorted_rows, perm = pl.pallas_call(
        send_rows_kernel,
        out_shape=(
            jax.ShapeDtypeStruct((tok_dev, heads_here * width), jnp.bfloat16),
            jax.ShapeDtypeStruct((heads_here, tok_dev, tok_dev), jnp.bfloat16),
        ),
    )(routes.T, *inputs)
    arrived = lax.all_to_all(sorted_rows, "seq", split_axis=0, concat_axis=0, tiled=True)

    pos = lax.broadcasted_iota(jnp.int32, (tok_dev,), 0)
    outs = []
    for h in range(heads_here):
        base = h * width
        cols = [arrived[:, base + i * HEAD_SIZE:base + (i + 1) * HEAD_SIZE] for i in range(n_in)]
        a, at = cluster_attend(*cols, pos)
        outs.append(jnp.concatenate([a, at], axis=1))
    back = jnp.concatenate(outs, axis=1)
    returned = lax.all_to_all(back, "seq", split_axis=0, concat_axis=0, tiled=True)

    local = pl.pallas_call(
        restore_kernel,
        out_shape=jax.ShapeDtypeStruct((2, tok_dev, heads_here * HEAD_SIZE), jnp.bfloat16),
    )(perm, returned)

    same = jnp.stack(
        [local]
        + [
            lax.ppermute(local, "yc", perm=[(i, (i + 2 * m) % n_g) for i in range(n_g)])
            for m in range(1, n_y)
        ],
        axis=1,
    )
    other = lax.ppermute(same, "yc", perm=[(i, i ^ 1) for i in range(n_g)])
    projected = jnp.einsum(
        "kcd,okic->odi", w_blocks[0], same, preferred_element_type=jnp.float32
    ) + jnp.einsum(
        "kcd,okic->odi", w_blocks[1], other, preferred_element_type=jnp.float32
    )
    mine = lax.dynamic_slice_in_dim(projected, zh * blk, blk, axis=1)
    theirs = lax.dynamic_slice_in_dim(projected, (1 - zh) * blk, blk, axis=1)
    other_half = lax.ppermute(theirs.astype(jnp.bfloat16), "zh", perm=[(0, 1), (1, 0)])
    summed = mine + other_half.astype(jnp.float32)
    return tuple(summed[o].T.astype(jnp.bfloat16) for o in range(2))


def solution(mesh):
    n_seq, n_ten = mesh.devices.shape
    split = Mesh(mesh.devices.reshape(n_seq, 2, n_ten // 2), ("seq", "zh", "yc"))
    rows = P("seq", ("zh", "yc"))
    return jax.shard_map(
        body,
        mesh=split,
        in_specs=(rows, rows, rows, rows, rows, rows, rows, P(("zh", "yc"), None)),
        out_specs=(rows, rows),
        check_vma=False,
    )
```

```python
import jax
import jax.numpy as jnp
from jax import lax
from jax.experimental import pallas as pl
from jax.sharding import Mesh, PartitionSpec as P

HEAD_SIZE = 128
CLUSTER = 256


def cluster_attend(q, k, v, dq, dk, dv, pos):
    scaling_multiplier = HEAD_SIZE ** (-0.5)
    logit_scores = (
        jnp.einsum("qe,ke->qk", q, k, preferred_element_type=jnp.float32) * scaling_multiplier
    )
    score_tangent_values = (
        jnp.einsum("qe,ke->qk", dq, k, preferred_element_type=jnp.float32)
        + jnp.einsum("qe,ke->qk", q, dk, preferred_element_type=jnp.float32)
    ) * scaling_multiplier
    visible = pos[None, :] <= pos[:, None]
    masked = jnp.where(visible, logit_scores, -jnp.inf)
    top_score = jnp.max(masked, axis=-1, keepdims=True)
    expo = jnp.where(visible, jnp.exp(masked - top_score), 0.0)
    attn_probs = expo / jnp.sum(expo, axis=-1, keepdims=True)
    probs_half = attn_probs.astype(jnp.bfloat16)
    attended_values = jnp.einsum(
        "qk,ke->qe", probs_half, v, preferred_element_type=jnp.float32
    ).astype(jnp.bfloat16)
    tangent_probs = attn_probs * (
        score_tangent_values - jnp.sum(attn_probs * score_tangent_values, axis=-1, keepdims=True)
    )
    tangent_half = tangent_probs.astype(jnp.bfloat16)
    attended_tangent_sum = (
        jnp.einsum("qk,ke->qe", tangent_half, v, preferred_element_type=jnp.float32)
        + jnp.einsum("qk,ke->qe", probs_half, dv, preferred_element_type=jnp.float32)
    ).astype(jnp.bfloat16)
    return attended_values, attended_tangent_sum


def send_rows_kernel(routes_t_ref, *refs):
    *ins, rows_ref, perm_ref = refs
    heads = routes_t_ref.shape[0]
    tok = routes_t_ref.shape[1]
    slots = lax.broadcasted_iota(jnp.int32, (tok, tok), 0)
    lanes = lax.broadcasted_iota(jnp.int32, (tok, tok), 1)
    for h in range(heads):
        cluster_row = routes_t_ref[h:h + 1, :] // CLUSTER
        cluster_col = jnp.sum(
            jnp.where(slots == lanes, cluster_row, 0), axis=1, keepdims=True
        )
        key_col = cluster_col * tok + slots[:, :1]
        key_row = cluster_row * tok + lanes[:1, :]
        less = key_col < key_row
        rank = jnp.sum(less.astype(jnp.int32), axis=0, keepdims=True)
        perm = (slots == rank).astype(jnp.bfloat16)
        perm_ref[h] = perm
        for m, x_ref in enumerate(ins):
            col = (h * len(ins) + m) * HEAD_SIZE
            rows_ref[:, col:col + HEAD_SIZE] = jnp.dot(
                perm, x_ref[:, h * HEAD_SIZE:(h + 1) * HEAD_SIZE],
                preferred_element_type=jnp.float32,
            ).astype(jnp.bfloat16)

def body(query_rows, key_rows, value_rows, query_tan, key_tan, value_tan, routes, out_weight):
    tok_dev = routes.shape[0]
    heads_here = routes.shape[1]
    n_seq = lax.axis_size("seq")
    inputs = (query_rows, key_rows, value_rows, query_tan, key_tan, value_tan)
    n_in = len(inputs)

    zh = lax.axis_index("zh")
    n_g = lax.axis_size("yc")
    blk = out_weight.shape[0]
    j_idx = lax.axis_index("yc")

    def cols_for(j):
        return jnp.concatenate(
            [
                lax.dynamic_slice_in_dim(out_weight, (zh * n_g + j) * blk, blk, axis=1),
                lax.dynamic_slice_in_dim(out_weight, ((1 - zh) * n_g + j) * blk, blk, axis=1),
            ],
            axis=1,
        )

    n_y = n_g // 2
    def pair_cols(j):
        return jnp.concatenate([cols_for(j), cols_for(jnp.bitwise_xor(j, 1))], axis=1)

    w_pairs = [pair_cols(j_idx)]
    for m in range(1, n_y):
        w_pairs.append(
            lax.ppermute(
                pair_cols((j_idx + 2 * m) % n_g),
                "yc",
                perm=[(i, (i + 2 * m) % n_g) for i in range(n_g)],
            )
        )
    w_same = [p[:, :2 * blk] for p in w_pairs]
    w_other = lax.ppermute(
        jnp.stack([p[:, 2 * blk:] for p in w_pairs]), "yc", perm=[(i, i ^ 1) for i in range(n_g)]
    )
    w_blocks = (jnp.stack(w_same), w_other)

    width = n_in * HEAD_SIZE
    sorted_rows, perm = pl.pallas_call(
        send_rows_kernel,
        out_shape=(
            jax.ShapeDtypeStruct((tok_dev, heads_here * width), jnp.bfloat16),
            jax.ShapeDtypeStruct((heads_here, tok_dev, tok_dev), jnp.bfloat16),
        ),
    )(routes.T, *inputs)
    arrived = lax.all_to_all(sorted_rows, "seq", split_axis=0, concat_axis=0, tiled=True)

    pos = lax.broadcasted_iota(jnp.int32, (tok_dev,), 0)
    outs = []
    for h in range(heads_here):
        base = h * width
        cols = [arrived[:, base + i * HEAD_SIZE:base + (i + 1) * HEAD_SIZE] for i in range(n_in)]
        a, at = cluster_attend(*cols, pos)
        outs.append(jnp.concatenate([a, at], axis=1))
    back = jnp.concatenate(outs, axis=1)
    returned = lax.all_to_all(back, "seq", split_axis=0, concat_axis=0, tiled=True)

    restored = [
        jnp.dot(
            perm[h].T,
            returned[:, h * 2 * HEAD_SIZE:(h + 1) * 2 * HEAD_SIZE],
            preferred_element_type=jnp.float32,
        ).astype(jnp.bfloat16)
        for h in range(heads_here)
    ]
    local = jnp.stack(
        [
            jnp.concatenate([r[:, o * HEAD_SIZE:(o + 1) * HEAD_SIZE] for r in restored], axis=1)
            for o in range(2)
        ]
    )

    flat = jnp.concatenate([local[0], local[1]], axis=1)
    same = jnp.stack(
        [flat]
        + [
            lax.ppermute(flat, "yc", perm=[(i, (i + 2 * m) % n_g) for i in range(n_g)])
            for m in range(1, n_y)
        ]
    )
    other = lax.ppermute(same, "yc", perm=[(i, i ^ 1) for i in range(n_g)])
    shape4 = (n_y, tok_dev, 2, heads_here * HEAD_SIZE)
    projected = jnp.einsum(
        "kcd,kioc->odi", w_blocks[0], same.reshape(shape4), preferred_element_type=jnp.float32
    ) + jnp.einsum(
        "kcd,kioc->odi", w_blocks[1], other.reshape(shape4), preferred_element_type=jnp.float32
    )
    mine = projected[:, :blk]
    theirs = projected[:, blk:]
    other_half = lax.ppermute(theirs.astype(jnp.bfloat16), "zh", perm=[(0, 1), (1, 0)])
    summed = mine + other_half.astype(jnp.float32)
    return tuple(summed[o].T.astype(jnp.bfloat16) for o in range(2))


def solution(mesh):
    n_seq, n_ten = mesh.devices.shape
    split = Mesh(mesh.devices.reshape(n_seq, 2, n_ten // 2), ("seq", "zh", "yc"))
    rows = P("seq", ("zh", "yc"))
    return jax.shard_map(
        body,
        mesh=split,
        in_specs=(rows, rows, rows, rows, rows, rows, rows, P(("zh", "yc"), None)),
        out_specs=(rows, rows),
        check_vma=False,
    )
```

```python
import jax
import jax.numpy as jnp
from jax import lax
from jax.experimental import pallas as pl
from jax.sharding import Mesh, PartitionSpec as P

HEAD_SIZE = 128
CLUSTER = 256


def cluster_attend(q, k, v, dq, dk, dv, pos):
    scaling_multiplier = HEAD_SIZE ** (-0.5)
    logit_scores = (
        jnp.einsum("qe,ke->qk", q, k, preferred_element_type=jnp.float32) * scaling_multiplier
    )
    score_tangent_values = (
        jnp.einsum("qe,ke->qk", dq, k, preferred_element_type=jnp.float32)
        + jnp.einsum("qe,ke->qk", q, dk, preferred_element_type=jnp.float32)
    ) * scaling_multiplier
    visible = pos[None, :] <= pos[:, None]
    masked = jnp.where(visible, logit_scores, -jnp.inf)
    top_score = jnp.max(masked, axis=-1, keepdims=True)
    expo = jnp.where(visible, jnp.exp(masked - top_score), 0.0)
    attn_probs = expo / jnp.sum(expo, axis=-1, keepdims=True)
    probs_half = attn_probs.astype(jnp.bfloat16)
    attended_values = jnp.einsum(
        "qk,ke->qe", probs_half, v, preferred_element_type=jnp.float32
    ).astype(jnp.bfloat16)
    tangent_probs = attn_probs * (
        score_tangent_values - jnp.sum(attn_probs * score_tangent_values, axis=-1, keepdims=True)
    )
    tangent_half = tangent_probs.astype(jnp.bfloat16)
    attended_tangent_sum = (
        jnp.einsum("qk,ke->qe", tangent_half, v, preferred_element_type=jnp.float32)
        + jnp.einsum("qk,ke->qe", probs_half, dv, preferred_element_type=jnp.float32)
    ).astype(jnp.bfloat16)
    return attended_values, attended_tangent_sum


def send_rows_kernel(routes_t_ref, *refs):
    *ins, rows_ref, perm_ref = refs
    heads = routes_t_ref.shape[0]
    tok = routes_t_ref.shape[1]
    slots = lax.broadcasted_iota(jnp.int32, (tok, tok), 0)
    lanes = lax.broadcasted_iota(jnp.int32, (tok, tok), 1)
    for h in range(heads):
        cluster_row = routes_t_ref[h:h + 1, :] // CLUSTER
        cluster_col = jnp.sum(
            jnp.where(slots == lanes, cluster_row, 0), axis=1, keepdims=True
        )
        key_col = cluster_col * tok + slots[:, :1]
        key_row = cluster_row * tok + lanes[:1, :]
        less = key_col < key_row
        rank = jnp.sum(less.astype(jnp.int32), axis=0, keepdims=True)
        perm = (slots == rank).astype(jnp.bfloat16)
        perm_ref[h] = perm
        for m, x_ref in enumerate(ins):
            col = (h * len(ins) + m) * HEAD_SIZE
            rows_ref[:, col:col + HEAD_SIZE] = jnp.dot(
                perm, x_ref[:, h * HEAD_SIZE:(h + 1) * HEAD_SIZE],
                preferred_element_type=jnp.float32,
            ).astype(jnp.bfloat16)

def body(query_rows, key_rows, value_rows, query_tan, key_tan, value_tan, routes, out_weight):
    tok_dev = routes.shape[0]
    heads_here = routes.shape[1]
    n_seq = lax.axis_size("seq")
    inputs = (query_rows, key_rows, value_rows, query_tan, key_tan, value_tan)
    n_in = len(inputs)

    zh = lax.axis_index("zh")
    n_g = lax.axis_size("yc")
    blk = out_weight.shape[0]
    j_idx = lax.axis_index("yc")

    def cols_for(j):
        return jnp.concatenate(
            [
                lax.dynamic_slice_in_dim(out_weight, (zh * n_g + j) * blk, blk, axis=1),
                lax.dynamic_slice_in_dim(out_weight, ((1 - zh) * n_g + j) * blk, blk, axis=1),
            ],
            axis=1,
        )

    n_y = n_g // 2
    def pair_cols(j):
        return jnp.concatenate([cols_for(j), cols_for(jnp.bitwise_xor(j, 1))], axis=1)

    w_pairs = [pair_cols(j_idx)]
    for m in range(1, n_y):
        w_pairs.append(
            lax.ppermute(
                pair_cols((j_idx + 2 * m) % n_g),
                "yc",
                perm=[(i, (i + 2 * m) % n_g) for i in range(n_g)],
            )
        )
    w_same = [p[:, :2 * blk] for p in w_pairs]
    w_other = lax.ppermute(
        jnp.stack([p[:, 2 * blk:] for p in w_pairs]), "yc", perm=[(i, i ^ 1) for i in range(n_g)]
    )
    w_blocks = (jnp.stack(w_same), w_other)

    width = n_in * HEAD_SIZE
    sorted_rows, perm = pl.pallas_call(
        send_rows_kernel,
        out_shape=(
            jax.ShapeDtypeStruct((tok_dev, heads_here * width), jnp.bfloat16),
            jax.ShapeDtypeStruct((heads_here, tok_dev, tok_dev), jnp.bfloat16),
        ),
    )(routes.T, *inputs)
    arrived = lax.all_to_all(sorted_rows, "seq", split_axis=0, concat_axis=0, tiled=True)

    pos = lax.broadcasted_iota(jnp.int32, (tok_dev,), 0)
    outs = []
    for h in range(heads_here):
        base = h * width
        cols = [arrived[:, base + i * HEAD_SIZE:base + (i + 1) * HEAD_SIZE] for i in range(n_in)]
        a, at = cluster_attend(*cols, pos)
        outs.append(jnp.concatenate([a, at], axis=1))
    back = jnp.concatenate(outs, axis=1)
    returned = lax.all_to_all(back, "seq", split_axis=0, concat_axis=0, tiled=True)

    restored = [
        jnp.dot(
            perm[h].T,
            returned[:, h * 2 * HEAD_SIZE:(h + 1) * 2 * HEAD_SIZE],
            preferred_element_type=jnp.float32,
        ).astype(jnp.bfloat16)
        for h in range(heads_here)
    ]
    local = jnp.stack(
        [
            jnp.concatenate([r[:, o * HEAD_SIZE:(o + 1) * HEAD_SIZE] for r in restored], axis=1)
            for o in range(2)
        ]
    )

    same = jnp.stack(
        [local]
        + [
            lax.ppermute(local, "yc", perm=[(i, (i + 2 * m) % n_g) for i in range(n_g)])
            for m in range(1, n_y)
        ],
        axis=1,
    )
    other = lax.ppermute(same, "yc", perm=[(i, i ^ 1) for i in range(n_g)])
    projected = jnp.einsum(
        "kcd,okic->odi", w_blocks[0], same, preferred_element_type=jnp.float32
    ) + jnp.einsum(
        "kcd,okic->odi", w_blocks[1], other, preferred_element_type=jnp.float32
    )
    mine = projected[:, :blk]
    theirs = projected[:, blk:]
    other_half = lax.ppermute(theirs.astype(jnp.bfloat16), "zh", perm=[(0, 1), (1, 0)])
    summed = mine + other_half.astype(jnp.float32)
    return tuple(summed[o].T.astype(jnp.bfloat16) for o in range(2))


def solution(mesh):
    n_seq, n_ten = mesh.devices.shape
    split = Mesh(mesh.devices.reshape(n_seq, 2, n_ten // 2), ("seq", "zh", "yc"))
    rows = P("seq", ("zh", "yc"))
    return jax.shard_map(
        body,
        mesh=split,
        in_specs=(rows, rows, rows, rows, rows, rows, rows, P(("zh", "yc"), None)),
        out_specs=(rows, rows),
        check_vma=False,
    )
```

```python
import jax
import jax.numpy as jnp
from jax import lax
from jax.experimental import pallas as pl
from jax.sharding import Mesh, PartitionSpec as P

HEAD_SIZE = 128
CLUSTER = 256


def cluster_attend(q, k, v, dq, dk, dv, pos):
    scaling_multiplier = HEAD_SIZE ** (-0.5)
    logit_scores = (
        jnp.einsum("qe,ke->qk", q, k, preferred_element_type=jnp.float32) * scaling_multiplier
    )
    score_tangent_values = (
        jnp.einsum("qe,ke->qk", dq, k, preferred_element_type=jnp.float32)
        + jnp.einsum("qe,ke->qk", q, dk, preferred_element_type=jnp.float32)
    ) * scaling_multiplier
    visible = pos[None, :] <= pos[:, None]
    masked = jnp.where(visible, logit_scores, -jnp.inf)
    top_score = jnp.max(masked, axis=-1, keepdims=True)
    expo = jnp.where(visible, jnp.exp(masked - top_score), 0.0)
    attn_probs = expo / jnp.sum(expo, axis=-1, keepdims=True)
    probs_half = attn_probs.astype(jnp.bfloat16)
    attended_values = jnp.einsum(
        "qk,ke->qe", probs_half, v, preferred_element_type=jnp.float32
    ).astype(jnp.bfloat16)
    tangent_probs = attn_probs * (
        score_tangent_values - jnp.sum(attn_probs * score_tangent_values, axis=-1, keepdims=True)
    )
    tangent_half = tangent_probs.astype(jnp.bfloat16)
    attended_tangent_sum = (
        jnp.einsum("qk,ke->qe", tangent_half, v, preferred_element_type=jnp.float32)
        + jnp.einsum("qk,ke->qe", probs_half, dv, preferred_element_type=jnp.float32)
    ).astype(jnp.bfloat16)
    return attended_values, attended_tangent_sum


def send_rows_kernel(routes_t_ref, *refs):
    *ins, rows_ref, perm_ref = refs
    heads = routes_t_ref.shape[0]
    tok = routes_t_ref.shape[1]
    slots = lax.broadcasted_iota(jnp.int32, (tok, tok), 0)
    lanes = lax.broadcasted_iota(jnp.int32, (tok, tok), 1)
    for h in range(heads):
        cluster_row = routes_t_ref[h:h + 1, :] // CLUSTER
        cluster_col = jnp.sum(
            jnp.where(slots == lanes, cluster_row, 0), axis=1, keepdims=True
        )
        key_col = cluster_col * tok + slots[:, :1]
        key_row = cluster_row * tok + lanes[:1, :]
        less = key_col < key_row
        rank = jnp.sum(less.astype(jnp.int32), axis=0, keepdims=True)
        perm = (slots == rank).astype(jnp.bfloat16)
        perm_ref[h] = perm
        for m, x_ref in enumerate(ins):
            col = (h * len(ins) + m) * HEAD_SIZE
            rows_ref[:, col:col + HEAD_SIZE] = jnp.dot(
                perm, x_ref[:, h * HEAD_SIZE:(h + 1) * HEAD_SIZE],
                preferred_element_type=jnp.float32,
            ).astype(jnp.bfloat16)

def body(query_rows, key_rows, value_rows, query_tan, key_tan, value_tan, routes, out_weight):
    tok_dev = routes.shape[0]
    heads_here = routes.shape[1]
    n_seq = lax.axis_size("seq")
    inputs = (query_rows, key_rows, value_rows, query_tan, key_tan, value_tan)
    n_in = len(inputs)

    zh = lax.axis_index("zh")
    n_g = lax.axis_size("yc")
    blk = out_weight.shape[0]
    j_idx = lax.axis_index("yc")

    def cols_for(j):
        return jnp.concatenate(
            [
                lax.dynamic_slice_in_dim(out_weight, (zh * n_g + j) * blk, blk, axis=1),
                lax.dynamic_slice_in_dim(out_weight, ((1 - zh) * n_g + j) * blk, blk, axis=1),
            ],
            axis=1,
        )

    n_y = n_g // 2
    def pair_cols(j):
        return jnp.concatenate([cols_for(j), cols_for(jnp.bitwise_xor(j, 1))], axis=1)

    w_pairs = [pair_cols(j_idx)]
    for m in range(1, n_y):
        w_pairs.append(
            lax.ppermute(
                pair_cols((j_idx + 2 * m) % n_g),
                "yc",
                perm=[(i, (i + 2 * m) % n_g) for i in range(n_g)],
            )
        )
    w_same = [p[:, :2 * blk] for p in w_pairs]
    w_other = lax.ppermute(
        jnp.stack([p[:, 2 * blk:] for p in w_pairs]), "yc", perm=[(i, i ^ 1) for i in range(n_g)]
    )
    w_blocks = (jnp.stack(w_same), w_other)

    width = n_in * HEAD_SIZE
    sorted_rows, perm = pl.pallas_call(
        send_rows_kernel,
        out_shape=(
            jax.ShapeDtypeStruct((tok_dev, heads_here * width), jnp.bfloat16),
            jax.ShapeDtypeStruct((heads_here, tok_dev, tok_dev), jnp.bfloat16),
        ),
    )(routes.T, *inputs)
    arrived = lax.all_to_all(sorted_rows, "seq", split_axis=0, concat_axis=0, tiled=True)

    pos = lax.broadcasted_iota(jnp.int32, (tok_dev,), 0)
    outs = []
    for h in range(heads_here):
        base = h * width
        cols = [arrived[:, base + i * HEAD_SIZE:base + (i + 1) * HEAD_SIZE] for i in range(n_in)]
        a, at = cluster_attend(*cols, pos)
        outs.append(jnp.concatenate([a, at], axis=1))
    back = jnp.concatenate(outs, axis=1)
    returned = lax.all_to_all(back, "seq", split_axis=0, concat_axis=0, tiled=True)

    local = jnp.einsum(
        "hki,khoe->oihe",
        perm,
        returned.reshape(tok_dev, heads_here, 2, HEAD_SIZE),
        preferred_element_type=jnp.float32,
    ).astype(jnp.bfloat16).reshape(2, tok_dev, heads_here * HEAD_SIZE)

    same = jnp.stack(
        [local]
        + [
            lax.ppermute(local, "yc", perm=[(i, (i + 2 * m) % n_g) for i in range(n_g)])
            for m in range(1, n_y)
        ],
        axis=1,
    )
    other = lax.ppermute(same, "yc", perm=[(i, i ^ 1) for i in range(n_g)])
    projected = jnp.einsum(
        "kcd,okic->odi", w_blocks[0], same, preferred_element_type=jnp.float32
    ) + jnp.einsum(
        "kcd,okic->odi", w_blocks[1], other, preferred_element_type=jnp.float32
    )
    mine = projected[:, :blk]
    theirs = projected[:, blk:]
    other_half = lax.ppermute(theirs.astype(jnp.bfloat16), "zh", perm=[(0, 1), (1, 0)])
    summed = mine + other_half.astype(jnp.float32)
    return tuple(summed[o].T.astype(jnp.bfloat16) for o in range(2))


def solution(mesh):
    n_seq, n_ten = mesh.devices.shape
    split = Mesh(mesh.devices.reshape(n_seq, 2, n_ten // 2), ("seq", "zh", "yc"))
    rows = P("seq", ("zh", "yc"))
    return jax.shard_map(
        body,
        mesh=split,
        in_specs=(rows, rows, rows, rows, rows, rows, rows, P(("zh", "yc"), None)),
        out_specs=(rows, rows),
        check_vma=False,
    )
```

```python
import jax
import jax.numpy as jnp
from jax import lax
from jax.experimental import pallas as pl
from jax.sharding import Mesh, PartitionSpec as P

HEAD_SIZE = 128
CLUSTER = 256


def cluster_attend(q, k, v, dq, dk, dv, pos):
    scaling_multiplier = HEAD_SIZE ** (-0.5)
    logit_scores = (
        jnp.einsum("qe,ke->qk", q, k, preferred_element_type=jnp.float32) * scaling_multiplier
    )
    score_tangent_values = (
        jnp.einsum("qe,ke->qk", dq, k, preferred_element_type=jnp.float32)
        + jnp.einsum("qe,ke->qk", q, dk, preferred_element_type=jnp.float32)
    ) * scaling_multiplier
    visible = pos[None, :] <= pos[:, None]
    masked = jnp.where(visible, logit_scores, -jnp.inf)
    top_score = jnp.max(masked, axis=-1, keepdims=True)
    expo = jnp.where(visible, jnp.exp(masked - top_score), 0.0)
    attn_probs = expo / jnp.sum(expo, axis=-1, keepdims=True)
    probs_half = attn_probs.astype(jnp.bfloat16)
    attended_values = jnp.einsum(
        "qk,ke->qe", probs_half, v, preferred_element_type=jnp.float32
    ).astype(jnp.bfloat16)
    tangent_probs = attn_probs * (
        score_tangent_values - jnp.sum(attn_probs * score_tangent_values, axis=-1, keepdims=True)
    )
    tangent_half = tangent_probs.astype(jnp.bfloat16)
    attended_tangent_sum = (
        jnp.einsum("qk,ke->qe", tangent_half, v, preferred_element_type=jnp.float32)
        + jnp.einsum("qk,ke->qe", probs_half, dv, preferred_element_type=jnp.float32)
    ).astype(jnp.bfloat16)
    return attended_values, attended_tangent_sum


def send_rows_kernel(routes_t_ref, *refs):
    *ins, rows_ref, perm_ref = refs
    heads = routes_t_ref.shape[0]
    tok = routes_t_ref.shape[1]
    slots = lax.broadcasted_iota(jnp.int32, (tok, tok), 0)
    lanes = lax.broadcasted_iota(jnp.int32, (tok, tok), 1)
    for h in range(heads):
        cluster_row = routes_t_ref[h:h + 1, :] // CLUSTER
        cluster_col = jnp.sum(
            jnp.where(slots == lanes, cluster_row, 0), axis=1, keepdims=True
        )
        key_col = cluster_col * tok + slots[:, :1]
        key_row = cluster_row * tok + lanes[:1, :]
        less = key_col < key_row
        rank = jnp.sum(less.astype(jnp.int32), axis=0, keepdims=True)
        perm = (slots == rank).astype(jnp.bfloat16)
        perm_ref[h] = perm
        for m, x_ref in enumerate(ins):
            col = (h * len(ins) + m) * HEAD_SIZE
            rows_ref[:, col:col + HEAD_SIZE] = jnp.dot(
                perm, x_ref[:, h * HEAD_SIZE:(h + 1) * HEAD_SIZE],
                preferred_element_type=jnp.float32,
            ).astype(jnp.bfloat16)

def body(query_rows, key_rows, value_rows, query_tan, key_tan, value_tan, routes, out_weight):
    tok_dev = routes.shape[0]
    heads_here = routes.shape[1]
    n_seq = lax.axis_size("seq")
    inputs = (query_rows, key_rows, value_rows, query_tan, key_tan, value_tan)
    n_in = len(inputs)

    zh = lax.axis_index("zh")
    n_g = lax.axis_size("yc")
    blk = out_weight.shape[0]
    j_idx = lax.axis_index("yc")

    def cols_for(j):
        return jnp.concatenate(
            [
                lax.dynamic_slice_in_dim(out_weight, (zh * n_g + j) * blk, blk, axis=1),
                lax.dynamic_slice_in_dim(out_weight, ((1 - zh) * n_g + j) * blk, blk, axis=1),
            ],
            axis=1,
        )

    n_y = n_g // 2
    def pair_cols(j):
        return jnp.concatenate([cols_for(j), cols_for(jnp.bitwise_xor(j, 1))], axis=1)

    w_pairs = [pair_cols(j_idx)]
    for m in range(1, n_y):
        w_pairs.append(
            lax.ppermute(
                pair_cols((j_idx + 2 * m) % n_g),
                "yc",
                perm=[(i, (i + 2 * m) % n_g) for i in range(n_g)],
            )
        )
    w_same = [p[:, :2 * blk] for p in w_pairs]
    w_other = lax.ppermute(
        jnp.stack([p[:, 2 * blk:] for p in w_pairs]), "yc", perm=[(i, i ^ 1) for i in range(n_g)]
    )
    w_blocks = (jnp.stack(w_same), w_other)

    width = n_in * HEAD_SIZE
    sorted_rows, perm = pl.pallas_call(
        send_rows_kernel,
        out_shape=(
            jax.ShapeDtypeStruct((tok_dev, heads_here * width), jnp.bfloat16),
            jax.ShapeDtypeStruct((heads_here, tok_dev, tok_dev), jnp.bfloat16),
        ),
    )(routes.T, *inputs)
    arrived = lax.all_to_all(sorted_rows, "seq", split_axis=0, concat_axis=0, tiled=True)

    pos = lax.broadcasted_iota(jnp.int32, (tok_dev,), 0)
    outs = []
    for h in range(heads_here):
        base = h * width
        cols = [arrived[:, base + i * HEAD_SIZE:base + (i + 1) * HEAD_SIZE] for i in range(n_in)]
        a, at = cluster_attend(*cols, pos)
        outs.append(jnp.concatenate([a, at], axis=1))
    back = jnp.concatenate(outs, axis=1)
    returned = lax.all_to_all(back, "seq", split_axis=0, concat_axis=0, tiled=True)

    restored = [
        jnp.dot(
            perm[h].T,
            returned[:, h * 2 * HEAD_SIZE:(h + 1) * 2 * HEAD_SIZE],
            preferred_element_type=jnp.float32,
        ).astype(jnp.bfloat16)
        for h in range(heads_here)
    ]
    local = jnp.stack(
        [
            jnp.concatenate([r[:, o * HEAD_SIZE:(o + 1) * HEAD_SIZE] for r in restored], axis=1)
            for o in range(2)
        ]
    )

    same = jnp.stack(
        [local]
        + [
            lax.ppermute(local, "yc", perm=[(i, (i + 2 * m) % n_g) for i in range(n_g)])
            for m in range(1, n_y)
        ],
        axis=1,
    )
    other = lax.ppermute(same, "yc", perm=[(i, i ^ 1) for i in range(n_g)])
    def project(part):
        cols = slice(part * blk, (part + 1) * blk)
        return jnp.einsum(
            "kcd,okic->odi", w_blocks[0][:, :, cols], same, preferred_element_type=jnp.float32
        ) + jnp.einsum(
            "kcd,okic->odi", w_blocks[1][:, :, cols], other, preferred_element_type=jnp.float32
        )

    theirs = project(1)
    other_half = lax.ppermute(theirs.astype(jnp.bfloat16), "zh", perm=[(0, 1), (1, 0)])
    mine = project(0)
    summed = mine + other_half.astype(jnp.float32)
    return tuple(summed[o].T.astype(jnp.bfloat16) for o in range(2))


def solution(mesh):
    n_seq, n_ten = mesh.devices.shape
    split = Mesh(mesh.devices.reshape(n_seq, 2, n_ten // 2), ("seq", "zh", "yc"))
    rows = P("seq", ("zh", "yc"))
    return jax.shard_map(
        body,
        mesh=split,
        in_specs=(rows, rows, rows, rows, rows, rows, rows, P(("zh", "yc"), None)),
        out_specs=(rows, rows),
        check_vma=False,
    )
```
